256 devices in a mesh: req: 32 (over z, x_hi, core), mlp: 8 (over x_lo, y).
Axes of the slice: x: 4 (x_hi: 2, x_lo: 2; x = x_hi * 2 + x_lo), y: 4, z: 8, core: 2. Of those that a mesh axis runs over, the one named last changes fastest.
Arguments:
- residual_in: bfloat16 [1024, 2560], P('req'), may hold values from -6 to 6
- queries: bfloat16 [1024, 2560], P('req', 'mlp')
- fresh_rotated_keys: bfloat16 [1024, 640], P('req', 'mlp'), may hold values from -6 to 6
- fresh_value_rows: bfloat16 [1024, 640], P('req', 'mlp'), may hold values from -6 to 6
- shared_prefix_keys: bfloat16 [32, 16384, 640], P(None, 'req', 'mlp'), may hold values from -6 to 6
- shared_prefix_values: bfloat16 [32, 16384, 640], P(None, 'req', 'mlp'), may hold values from -6 to 6
- sample_tail_keys: bfloat16 [32, 16, 128, 640], P('req', None, None, 'mlp'), may hold values from -6 to 6
- sample_tail_values: bfloat16 [32, 16, 128, 640], P('req', None, None, 'mlp'), may hold values from -6 to 6
- prompt_prefix_length: int32 [32], replicated, may hold values from 1 to 16384, as said below
- sample_tail_length: int32 [32, 16], P('req'), may hold values from 0 to 128, as said below
- out_weight: bfloat16 [2560, 2560], P('mlp'), may hold values from -0.125 to 0.125
- gate_weight: bfloat16 [2560, 4096], P(None, 'mlp'), may hold values from -0.125 to 0.125
- up_weight: bfloat16 [2560, 4096], P(None, 'mlp'), may hold values from -0.125 to 0.125
- down_weight: bfloat16 [4096, 2560], P('mlp'), may hold values from -0.09375 to 0.09375
- mlp_gain: float32 [2560], replicated, may hold values from 0.1 to 1.9
- final_gain: float32 [2560], replicated, may hold values from 0.1 to 1.9
- score_weight: float32 [2560], replicated, may hold values from -0.125 to 0.125
Outputs:
- layer_out: bfloat16 [1024, 2560], P('req', 'mlp')
- score: float32 [1024], P('req')
The draws below stay inside these ranges and needn't reach their ends.
Inputs may be any that keep to these rules, and one draw needn't show every extreme that they name: `prompt_prefix_length`: one prompt in every draw has the full prefix length 16384. `sample_tail_length`: one sample in every draw has the full tail length 128.
All inputs are finite; a program needn't handle non-finite values.
Results may differ from the reference program's by a relative error of at most 0.02.
Values may be sent and summed in bfloat16 or wider, within the bound.
No kernel may reach another device: no remote copies, remote signals or barrier semaphores. Data moves between devices by JAX's collectives and lax.ppermute only.
A program may use at most 128 MiB of HBM per device.

```python
import jax
import jax.numpy as jnp
from jax import lax

D = 2560
QUERY_HEADS = 32
KEY_VALUE_HEADS = 8
HEAD_SIZE = 80
FF = 4096
SAMPLE_COUNT = 16
DECODE_TOKENS = 2
TAIL_LENGTH = 128
PROMPT_COUNT = 32
PREFIX_LENGTH = 16384
TOKEN_COUNT = 1024


def draw_queries(key, part):
    first_key = jax.random.fold_in(jax.random.fold_in(key, 11), 0)
    values = 3.0 * jax.random.normal(first_key, (TOKEN_COUNT, QUERY_HEADS * HEAD_SIZE), jnp.float32)
    return values.astype(jnp.bfloat16)


def draw_prompt_prefix_length(key, part):
    first_key, second_key = jax.random.split(jax.random.fold_in(key, 21))
    lengths = jax.random.randint(first_key, (PROMPT_COUNT,), 1, PREFIX_LENGTH + 1)
    chosen = jax.random.randint(second_key, (), 0, PROMPT_COUNT)
    return lengths.at[chosen].set(PREFIX_LENGTH).astype(jnp.int32)


def draw_sample_tail_length(key, part):
    first_key, second_key = jax.random.split(jax.random.fold_in(key, 31))
    lengths = jax.random.randint(first_key, (PROMPT_COUNT * SAMPLE_COUNT,), 0, TAIL_LENGTH + 1)
    chosen = jax.random.randint(second_key, (), 0, PROMPT_COUNT * SAMPLE_COUNT)
    return lengths.at[chosen].set(TAIL_LENGTH).astype(jnp.int32).reshape(PROMPT_COUNT, SAMPLE_COUNT)


def steps_of(key, dims, cuts, least, top_value):
    def one(dim, shards_of):
        draws = jax.random.uniform(jax.random.fold_in(jax.random.fold_in(key, 6), dim), (shards_of,), jnp.float32, least / len(cuts), top_value / len(cuts))
        return jnp.repeat(jnp.exp(draws), dims[dim] // shards_of).reshape((-1,) + (1,) * (len(dims) - dim - 1))

    level = one(*cuts[0])
    for cut in cuts[1:]:
        level = level * one(*cut)
    return level


def gaussian(own_key, shape, deviation, bound, shards=(), held_as=jnp.bfloat16):
    gain = steps_of(own_key, shape, shards, -0.22, 0.18) if shards else 1.0
    entries = jax.random.normal(own_key, shape, jnp.float32) * deviation * gain
    return jnp.minimum(jnp.maximum(entries, -bound), bound).astype(held_as)


def setup_inputs(seed: int = 0) -> dict:
    splits = jax.random.split(jax.random.key(seed), 18)
    residual_in = gaussian(splits[0], (TOKEN_COUNT, D), 1.0, 6.0, ((0, 32),))
    queries = draw_queries(jax.random.fold_in(splits[17], 71), 0)
    fresh_rotated_keys = gaussian(splits[2], (TOKEN_COUNT, KEY_VALUE_HEADS * HEAD_SIZE), 1.0, 6.0, ((0, 32), (1, 8)))
    fresh_value_rows = gaussian(splits[3], (TOKEN_COUNT, KEY_VALUE_HEADS * HEAD_SIZE), 1.0, 6.0, ((0, 32), (1, 8)))
    shared_prefix_keys = gaussian(splits[4], (PROMPT_COUNT, PREFIX_LENGTH, KEY_VALUE_HEADS * HEAD_SIZE), 1.0, 6.0, ((1, 32), (2, 8)))
    shared_prefix_values = gaussian(splits[5], (PROMPT_COUNT, PREFIX_LENGTH, KEY_VALUE_HEADS * HEAD_SIZE), 1.0, 6.0, ((1, 32), (2, 8)))
    sample_tail_keys = gaussian(splits[6], (PROMPT_COUNT, SAMPLE_COUNT, TAIL_LENGTH, KEY_VALUE_HEADS * HEAD_SIZE), 1.0, 6.0, ((0, 32), (3, 8)))
    sample_tail_values = gaussian(splits[7], (PROMPT_COUNT, SAMPLE_COUNT, TAIL_LENGTH, KEY_VALUE_HEADS * HEAD_SIZE), 1.0, 6.0, ((0, 32), (3, 8)))
    prompt_prefix_length = draw_prompt_prefix_length(jax.random.fold_in(splits[17], 71), 0)
    sample_tail_length = draw_sample_tail_length(jax.random.fold_in(splits[17], 71), 0)
    out_weight = gaussian(splits[10], (QUERY_HEADS * HEAD_SIZE, D), (QUERY_HEADS * HEAD_SIZE) ** -0.5, 0.125, ((0, 8),))
    gate_weight = gaussian(splits[11], (D, FF), D ** -0.5, 0.125, ((1, 8),))
    up_weight = gaussian(splits[12], (D, FF), D ** -0.5, 0.125, ((1, 8),))
    down_weight = gaussian(splits[13], (FF, D), FF ** -0.5, 0.09375, ((0, 8),))
    mlp_gain = jnp.clip(1.0 + 0.18 * jax.random.normal(splits[14], (D,), jnp.float32), 0.1, 1.9)
    final_gain = jnp.clip(1.0 + 0.18 * jax.random.normal(splits[15], (D,), jnp.float32), 0.1, 1.9)
    score_weight = gaussian(splits[16], (D,), D ** -0.5, 0.125, (), jnp.float32)
    return dict(residual_in=residual_in, queries=queries, fresh_rotated_keys=fresh_rotated_keys, fresh_value_rows=fresh_value_rows, shared_prefix_keys=shared_prefix_keys, shared_prefix_values=shared_prefix_values, sample_tail_keys=sample_tail_keys, sample_tail_values=sample_tail_values, prompt_prefix_length=prompt_prefix_length, sample_tail_length=sample_tail_length, out_weight=out_weight, gate_weight=gate_weight, up_weight=up_weight, down_weight=down_weight, mlp_gain=mlp_gain, final_gain=final_gain, score_weight=score_weight)


def single_prompt(items):
    query_matrix, fresh_key_block, fresh_value_block, prefix_key_block, prefix_value_block, tail_key_block, tail_value_block, plen, tlen = items
    query_groups = QUERY_HEADS // KEY_VALUE_HEADS
    inv_root = HEAD_SIZE ** (-0.5)
    query_grouped = query_matrix.astype(jnp.float32).reshape(SAMPLE_COUNT, DECODE_TOKENS, KEY_VALUE_HEADS, query_groups, HEAD_SIZE)
    prefix_key_flat = prefix_key_block.astype(jnp.float32).reshape(PREFIX_LENGTH, KEY_VALUE_HEADS, HEAD_SIZE)
    prefix_value_flat = prefix_value_block.astype(jnp.float32).reshape(PREFIX_LENGTH, KEY_VALUE_HEADS, HEAD_SIZE)
    tail_key_flat = tail_key_block.astype(jnp.float32).reshape(SAMPLE_COUNT, TAIL_LENGTH, KEY_VALUE_HEADS, HEAD_SIZE)
    tail_value_flat = tail_value_block.astype(jnp.float32).reshape(SAMPLE_COUNT, TAIL_LENGTH, KEY_VALUE_HEADS, HEAD_SIZE)
    fresh_key_flat = fresh_key_block.astype(jnp.float32).reshape(SAMPLE_COUNT, DECODE_TOKENS, KEY_VALUE_HEADS, HEAD_SIZE)
    fresh_value_flat = fresh_value_block.astype(jnp.float32).reshape(SAMPLE_COUNT, DECODE_TOKENS, KEY_VALUE_HEADS, HEAD_SIZE)
    score_pre = jnp.einsum('sjkgh,lkh->sjkgl', query_grouped, prefix_key_flat) * inv_root
    score_tail = jnp.einsum('sjkgh,stkh->sjkgt', query_grouped, tail_key_flat) * inv_root
    score_new = jnp.einsum('sjkgh,sikh->sjkgi', query_grouped, fresh_key_flat) * inv_root
    mask_pre = (jnp.arange(PREFIX_LENGTH) < plen)[None, None, None, None, :]
    mask_tail = (jnp.arange(TAIL_LENGTH)[None, :] < tlen[:, None])[:, None, None, None, :]
    causal = (jnp.arange(DECODE_TOKENS)[None, :] <= jnp.arange(DECODE_TOKENS)[:, None])[None, :, None, None, :]
    low = jnp.float32(-1e+30)
    top = jnp.maximum(lax.optimization_barrier(jnp.max(jnp.where(mask_pre, score_pre, low), -1)), lax.optimization_barrier(jnp.max(jnp.where(mask_tail, score_tail, low), -1)))
    top = jnp.maximum(top, lax.optimization_barrier(jnp.max(jnp.where(causal, score_new, low), -1)))
    w_pre = jnp.where(mask_pre, jnp.exp(score_pre - top[..., None]), 0.0)
    w_tail = jnp.where(mask_tail, jnp.exp(score_tail - top[..., None]), 0.0)
    w_new = jnp.where(causal, jnp.exp(score_new - top[..., None]), 0.0)
    total = lax.optimization_barrier(jnp.sum(w_pre, -1)) + lax.optimization_barrier(jnp.sum(w_tail, -1)) + lax.optimization_barrier(jnp.sum(w_new, -1))
    numer = jnp.einsum('sjkgl,lkh->sjkgh', w_pre.astype(jnp.bfloat16).astype(jnp.float32), prefix_value_flat)
    numer = numer + jnp.einsum('sjkgt,stkh->sjkgh', w_tail.astype(jnp.bfloat16).astype(jnp.float32), tail_value_flat)
    numer = numer + jnp.einsum('sjkgi,sikh->sjkgh', w_new.astype(jnp.bfloat16).astype(jnp.float32), fresh_value_flat)
    result = (numer / total[..., None]).astype(jnp.bfloat16)
    return result.reshape(SAMPLE_COUNT * DECODE_TOKENS, QUERY_HEADS * HEAD_SIZE)

def reference(residual_in, queries, fresh_rotated_keys, fresh_value_rows, shared_prefix_keys, shared_prefix_values, sample_tail_keys, sample_tail_values, prompt_prefix_length, sample_tail_length, out_weight, gate_weight, up_weight, down_weight, mlp_gain, final_gain, score_weight):
    token_rows = SAMPLE_COUNT * DECODE_TOKENS
    attention_layer = lax.map(single_prompt, (queries.reshape(PROMPT_COUNT, token_rows, QUERY_HEADS * HEAD_SIZE), fresh_rotated_keys.reshape(PROMPT_COUNT, token_rows, KEY_VALUE_HEADS * HEAD_SIZE), fresh_value_rows.reshape(PROMPT_COUNT, token_rows, KEY_VALUE_HEADS * HEAD_SIZE), shared_prefix_keys, shared_prefix_values, sample_tail_keys, sample_tail_values, prompt_prefix_length, sample_tail_length))
    attention_layer = attention_layer.reshape(TOKEN_COUNT, QUERY_HEADS * HEAD_SIZE)
    mid = residual_in.astype(jnp.float32) + jnp.dot(attention_layer, out_weight, preferred_element_type=jnp.float32)
    normed = (mid * lax.rsqrt(lax.optimization_barrier(jnp.mean(mid * mid, -1, keepdims=True)) + 1e-05) * mlp_gain).astype(jnp.bfloat16)
    gate = jnp.dot(normed, gate_weight, preferred_element_type=jnp.float32)
    upper = jnp.dot(normed, up_weight, preferred_element_type=jnp.float32)
    hidden = (jax.nn.silu(gate) * upper).astype(jnp.bfloat16)
    stream = mid + jnp.dot(hidden, down_weight, preferred_element_type=jnp.float32)
    score = lax.optimization_barrier(jnp.sum(stream * lax.rsqrt(lax.optimization_barrier(jnp.mean(stream * stream, -1, keepdims=True)) + 1e-05) * final_gain * score_weight, -1))
    return (stream.astype(jnp.bfloat16), score)
```

```python
import jax
import jax.numpy as jnp
from jax import lax
from jax.sharding import PartitionSpec as P

D = 2560
QUERY_HEADS = 32
KEY_VALUE_HEADS = 8
HEAD_SIZE = 80
SAMPLE_COUNT = 16
DECODE_TOKENS = 2
TAIL_LENGTH = 128


def rms_scale(total_sq, width):
    return lax.rsqrt(total_sq / width + 1e-05)


def exchange(x, axis, n, bit):
    return lax.ppermute(x, axis, perm=[(i, i ^ (1 << bit)) for i in range(n)])


def gather_rows(x, axis, n, bits):
    me = lax.axis_index(axis)
    buf = x[None]
    taken = []
    for b in bits:
        other = exchange(buf, axis, n, b)
        high = ((me >> b) & 1) == 1
        buf = jnp.stack([jnp.where(high, other, buf), jnp.where(high, buf, other)])
        taken.insert(0, b)
    nb = len(bits)
    order = sorted(range(nb), key=lambda i: -taken[i])
    buf = jnp.transpose(buf, order + list(range(nb, buf.ndim)))
    return buf.reshape((n * x.shape[0],) + x.shape[1:])


def merge_partials(a, b):
    ma = a[..., HEAD_SIZE:HEAD_SIZE + 1, :]
    mb = b[..., HEAD_SIZE:HEAD_SIZE + 1, :]
    top = jnp.maximum(ma, mb)
    wa = jnp.exp(ma - top)
    wb = jnp.exp(mb - top)
    outs = a[..., :HEAD_SIZE, :] * wa + b[..., :HEAD_SIZE, :] * wb
    sums = a[..., HEAD_SIZE + 1:, :] * wa + b[..., HEAD_SIZE + 1:, :] * wb
    return jnp.concatenate([outs, top, sums], axis=-2)


def reduce_partials(packed, axis, n, bits):
    me = lax.axis_index(axis)
    nb = len(bits)
    cur = packed.reshape((2,) * nb + packed.shape[1:])
    left = list(range(nb - 1, -1, -1))
    for b in bits:
        ax = left.index(b)
        own = (me >> b) & 1
        keep = lax.dynamic_index_in_dim(cur, own, ax, keepdims=False)
        send = lax.dynamic_index_in_dim(cur, 1 - own, ax, keepdims=False)
        cur = merge_partials(keep, exchange(send, axis, n, b))
        left.remove(b)
    return cur


def allreduce_bf16(x, axis, n, bits):
    cur = x.astype(jnp.bfloat16)
    for b in bits:
        other = exchange(cur, axis, n, b)
        cur = (cur.astype(jnp.float32) + other.astype(jnp.float32)).astype(jnp.bfloat16)
    return cur


def on_device(
    residual_in,
    queries,
    fresh_rotated_keys,
    fresh_value_rows,
    shared_prefix_keys,
    shared_prefix_values,
    sample_tail_keys,
    sample_tail_values,
    prompt_prefix_length,
    sample_tail_length,
    out_weight,
    gate_weight,
    up_weight,
    down_weight,
    mlp_gain,
    final_gain,
    score_weight,
):
    query_groups = QUERY_HEADS // KEY_VALUE_HEADS
    inv_root = HEAD_SIZE ** (-0.5)
    kv_local = fresh_rotated_keys.shape[1] // HEAD_SIZE
    prompts = shared_prefix_keys.shape[0]
    piece_len = shared_prefix_keys.shape[1]
    req_count = lax.axis_size("req")
    req_bits = req_count.bit_length() - 1
    mlp_count = lax.axis_size("mlp")
    mlp_bits = mlp_count.bit_length() - 1
    req_index = lax.axis_index("req")
    low = jnp.float32(-1e30)
    rows = kv_local * SAMPLE_COUNT * DECODE_TOKENS * query_groups

    gather_order = [req_bits - 1] + ([1] if req_bits > 1 else []) + list(range(req_bits - 2, 1, -1)) + [0]
    gather_order = [b for i, b in enumerate(gather_order) if b not in gather_order[:i]]
    reduce_order = gather_order[::-1]

    gathered = gather_rows(queries, "req", req_count, gather_order)
    query_all = gathered.reshape(
        prompts, SAMPLE_COUNT, DECODE_TOKENS, kv_local, query_groups, HEAD_SIZE
    )
    prefix_key_block = shared_prefix_keys.reshape(prompts, piece_len, kv_local, HEAD_SIZE)
    prefix_value_block = shared_prefix_values.reshape(prompts, piece_len, kv_local, HEAD_SIZE)
    score_pre = (
        jnp.einsum(
            "psjkgh,plkh->pksjgl", query_all, prefix_key_block, preferred_element_type=jnp.float32
        )
        * inv_root
    )
    key_place = req_index * piece_len + jnp.arange(piece_len)
    valid = (key_place[None, :] < prompt_prefix_length[:, None])[:, None, None, None, None, :]
    piece_top = jnp.max(jnp.where(valid, score_pre, low), -1)
    piece_w = jnp.where(valid, jnp.exp(score_pre - piece_top[..., None]), 0.0)
    piece_sum = jnp.sum(piece_w, -1)
    piece_out = jnp.einsum(
        "pksjgl,plkh->phksjg",
        piece_w.astype(jnp.bfloat16),
        prefix_value_block,
        preferred_element_type=jnp.float32,
    )
    packed = jnp.concatenate(
        [
            piece_out.reshape(prompts, HEAD_SIZE, rows),
            piece_top.reshape(prompts, 1, rows),
            piece_sum.reshape(prompts, 1, rows),
        ],
        axis=1,
    )
    own_part = reduce_partials(packed, "req", req_count, reduce_order)

    query_own = queries.reshape(SAMPLE_COUNT, DECODE_TOKENS, kv_local, query_groups, HEAD_SIZE)
    tail_key_block = sample_tail_keys.reshape(SAMPLE_COUNT, TAIL_LENGTH, kv_local, HEAD_SIZE)
    tail_value_block = sample_tail_values.reshape(SAMPLE_COUNT, TAIL_LENGTH, kv_local, HEAD_SIZE)
    fresh_k = fresh_rotated_keys.reshape(SAMPLE_COUNT, DECODE_TOKENS, kv_local, HEAD_SIZE)
    fresh_v = fresh_value_rows.reshape(SAMPLE_COUNT, DECODE_TOKENS, kv_local, HEAD_SIZE)
    score_tail = (
        jnp.einsum(
            "sjkgh,stkh->ksjgt", query_own, tail_key_block, preferred_element_type=jnp.float32
        )
        * inv_root
    )
    score_new = (
        jnp.einsum("sjkgh,sikh->ksjgi", query_own, fresh_k, preferred_element_type=jnp.float32)
        * inv_root
    )
    mask_tail = (jnp.arange(TAIL_LENGTH)[None, :] < sample_tail_length[0][:, None])[
        None, :, None, None, :
    ]
    causal = (jnp.arange(DECODE_TOKENS)[None, :] <= jnp.arange(DECODE_TOKENS)[:, None])[
        None, None, :, None, :
    ]
    local_top = jnp.maximum(
        jnp.max(jnp.where(mask_tail, score_tail, low), -1),
        jnp.max(jnp.where(causal, score_new, low), -1),
    )
    w_tail = jnp.where(mask_tail, jnp.exp(score_tail - local_top[..., None]), 0.0)
    w_new = jnp.where(causal, jnp.exp(score_new - local_top[..., None]), 0.0)
    local_sum = jnp.sum(w_tail, -1) + jnp.sum(w_new, -1)
    local_out = jnp.einsum(
        "ksjgt,stkh->ksjgh",
        w_tail.astype(jnp.bfloat16),
        tail_value_block,
        preferred_element_type=jnp.float32,
    )
    local_out = local_out + jnp.einsum(
        "ksjgi,sikh->ksjgh", w_new.astype(jnp.bfloat16), fresh_v, preferred_element_type=jnp.float32
    )
    lead = (kv_local, SAMPLE_COUNT, DECODE_TOKENS, query_groups)
    source_out = jnp.transpose(own_part[:HEAD_SIZE].reshape((HEAD_SIZE,) + lead), (1, 2, 3, 4, 0))
    source_top = own_part[HEAD_SIZE].reshape(lead)
    source_sum = own_part[HEAD_SIZE + 1].reshape(lead)
    overall = jnp.maximum(source_top, local_top)
    source_w = jnp.exp(source_top - overall)
    local_w = jnp.exp(local_top - overall)
    numer = source_w[..., None] * source_out + local_w[..., None] * local_out
    denom = source_w * source_sum + local_w * local_sum
    attention_layer = (numer / denom[..., None]).astype(jnp.bfloat16)
    attention_layer = jnp.transpose(attention_layer, (1, 2, 0, 3, 4)).reshape(
        SAMPLE_COUNT * DECODE_TOKENS, kv_local * query_groups * HEAD_SIZE
    )
    projected = jnp.dot(attention_layer, out_weight, preferred_element_type=jnp.float32)
    mlp_index = lax.axis_index("mlp")
    share = D // mlp_count
    mlp_order = list(range(mlp_bits - 1, -1, -1))
    mid = residual_in.astype(jnp.float32) + allreduce_bf16(
        projected, "mlp", mlp_count, mlp_order
    ).astype(jnp.float32)
    normed = (mid * rms_scale(jnp.sum(mid * mid, -1, keepdims=True), D) * mlp_gain).astype(
        jnp.bfloat16
    )
    gate = jnp.dot(normed, gate_weight, preferred_element_type=jnp.float32)
    upper = jnp.dot(normed, up_weight, preferred_element_type=jnp.float32)
    hidden = (jax.nn.silu(gate) * upper).astype(jnp.bfloat16)
    stream = mid + allreduce_bf16(
        jnp.dot(hidden, down_weight, preferred_element_type=jnp.float32), "mlp", mlp_count, mlp_order
    ).astype(jnp.float32)
    score = jnp.sum(
        stream
        * rms_scale(jnp.sum(stream * stream, -1, keepdims=True), D)
        * final_gain
        * score_weight,
        -1,
    )
    layer_out = lax.dynamic_slice_in_dim(stream, mlp_index * share, share, 1).astype(jnp.bfloat16)
    return (layer_out, score)


def solution(mesh):
    placed = (
        P("req", None),
        P("req", "mlp"),
        P("req", "mlp"),
        P("req", "mlp"),
        P(None, "req", "mlp"),
        P(None, "req", "mlp"),
        P("req", None, None, "mlp"),
        P("req", None, None, "mlp"),
        P(),
        P("req", None),
        P("mlp", None),
        P(None, "mlp"),
        P(None, "mlp"),
        P("mlp", None),
        P(),
        P(),
        P(),
    )
    return jax.shard_map(
        on_device,
        mesh=mesh,
        in_specs=placed,
        out_specs=(P("req", "mlp"), P("req")),
        check_vma=False,
    )
```

```python
import jax
import jax.numpy as jnp
from jax import lax
from jax.sharding import PartitionSpec as P

D = 2560
QUERY_HEADS = 32
KEY_VALUE_HEADS = 8
HEAD_SIZE = 80
SAMPLE_COUNT = 16
DECODE_TOKENS = 2
TAIL_LENGTH = 128


def rms_scale(total_sq, width):
    return lax.rsqrt(total_sq / width + 1e-05)


def shifted(x, axis, n, s):
    return lax.ppermute(x, axis, perm=[(i, (i + s) % n) for i in range(n)])


def roll_lead(x, shift, n):
    both = jnp.concatenate([x, x], axis=0)
    return lax.dynamic_slice_in_dim(both, (n - shift) % n, n, 0)


def gather_all(x, axis, n):
    me = lax.axis_index(axis)
    got = [x] + [shifted(x, axis, n, (n - s) % n) for s in range(1, n)]
    return roll_lead(jnp.stack(got), me, n)


def scatter_all(x, axis, n):
    me = lax.axis_index(axis)
    mine = roll_lead(x, (n - me) % n, n)
    got = [mine[0]] + [shifted(mine[s], axis, n, s) for s in range(1, n)]
    return roll_lead(jnp.stack(got)[::-1], (me + 1) % n, n)


def sum_all(x, axis, n):
    part = x.astype(jnp.bfloat16)
    got = [part] + [shifted(part, axis, n, s) for s in range(1, n)]
    me = lax.axis_index(axis)
    ordered = roll_lead(jnp.stack(got)[::-1], (me + 1) % n, n)
    total = ordered[0].astype(jnp.float32)
    for i in range(1, n):
        total = total + ordered[i].astype(jnp.float32)
    return total


def merge_sources(parts):
    tops = parts[:, HEAD_SIZE, :]
    top = jnp.max(tops, 0)
    w = jnp.exp(tops - top[None])
    outs = jnp.sum(parts[:, :HEAD_SIZE, :] * w[:, None, :], 0)
    sums = jnp.sum(parts[:, HEAD_SIZE + 1, :] * w, 0)
    return outs, top, sums


def on_device(
    residual_in,
    queries,
    fresh_rotated_keys,
    fresh_value_rows,
    shared_prefix_keys,
    shared_prefix_values,
    sample_tail_keys,
    sample_tail_values,
    prompt_prefix_length,
    sample_tail_length,
    out_weight,
    gate_weight,
    up_weight,
    down_weight,
    mlp_gain,
    final_gain,
    score_weight,
):
    query_groups = QUERY_HEADS // KEY_VALUE_HEADS
    inv_root = HEAD_SIZE ** (-0.5)
    kv_local = fresh_rotated_keys.shape[1] // HEAD_SIZE
    prompts = shared_prefix_keys.shape[0]
    piece_len = shared_prefix_keys.shape[1]
    req_count = lax.axis_size("req")
    mlp_count = lax.axis_size("mlp")
    req_index = lax.axis_index("req")
    low = jnp.float32(-1e30)
    rows = kv_local * SAMPLE_COUNT * DECODE_TOKENS * query_groups

    gathered = gather_all(queries, "req", req_count)
    query_all = gathered.reshape(
        prompts, SAMPLE_COUNT, DECODE_TOKENS, kv_local, query_groups, HEAD_SIZE
    )
    prefix_key_block = shared_prefix_keys.reshape(prompts, piece_len, kv_local, HEAD_SIZE)
    prefix_value_block = shared_prefix_values.reshape(prompts, piece_len, kv_local, HEAD_SIZE)
    score_pre = (
        jnp.einsum(
            "psjkgh,plkh->pksjgl", query_all, prefix_key_block, preferred_element_type=jnp.float32
        )
        * inv_root
    )
    key_place = req_index * piece_len + jnp.arange(piece_len)
    valid = (key_place[None, :] < prompt_prefix_length[:, None])[:, None, None, None, None, :]
    piece_top = jnp.max(jnp.where(valid, score_pre, low), -1)
    piece_w = jnp.where(valid, jnp.exp(score_pre - piece_top[..., None]), 0.0)
    piece_sum = jnp.sum(piece_w, -1)
    piece_out = jnp.einsum(
        "pksjgl,plkh->phksjg",
        piece_w.astype(jnp.bfloat16),
        prefix_value_block,
        preferred_element_type=jnp.float32,
    )
    packed = jnp.concatenate(
        [
            piece_out.reshape(prompts, HEAD_SIZE, rows),
            piece_top.reshape(prompts, 1, rows),
            piece_sum.reshape(prompts, 1, rows),
        ],
        axis=1,
    )
    source_out, source_top, source_sum = merge_sources(scatter_all(packed, "req", req_count))

    query_own = queries.reshape(SAMPLE_COUNT, DECODE_TOKENS, kv_local, query_groups, HEAD_SIZE)
    tail_key_block = sample_tail_keys.reshape(SAMPLE_COUNT, TAIL_LENGTH, kv_local, HEAD_SIZE)
    tail_value_block = sample_tail_values.reshape(SAMPLE_COUNT, TAIL_LENGTH, kv_local, HEAD_SIZE)
    fresh_k = fresh_rotated_keys.reshape(SAMPLE_COUNT, DECODE_TOKENS, kv_local, HEAD_SIZE)
    fresh_v = fresh_value_rows.reshape(SAMPLE_COUNT, DECODE_TOKENS, kv_local, HEAD_SIZE)
    score_tail = (
        jnp.einsum(
            "sjkgh,stkh->ksjgt", query_own, tail_key_block, preferred_element_type=jnp.float32
        )
        * inv_root
    )
    score_new = (
        jnp.einsum("sjkgh,sikh->ksjgi", query_own, fresh_k, preferred_element_type=jnp.float32)
        * inv_root
    )
    mask_tail = (jnp.arange(TAIL_LENGTH)[None, :] < sample_tail_length[0][:, None])[
        None, :, None, None, :
    ]
    causal = (jnp.arange(DECODE_TOKENS)[None, :] <= jnp.arange(DECODE_TOKENS)[:, None])[
        None, None, :, None, :
    ]
    local_top = jnp.maximum(
        jnp.max(jnp.where(mask_tail, score_tail, low), -1),
        jnp.max(jnp.where(causal, score_new, low), -1),
    )
    w_tail = jnp.where(mask_tail, jnp.exp(score_tail - local_top[..., None]), 0.0)
    w_new = jnp.where(causal, jnp.exp(score_new - local_top[..., None]), 0.0)
    local_sum = jnp.sum(w_tail, -1) + jnp.sum(w_new, -1)
    local_out = jnp.einsum(
        "ksjgt,stkh->ksjgh",
        w_tail.astype(jnp.bfloat16),
        tail_value_block,
        preferred_element_type=jnp.float32,
    )
    local_out = local_out + jnp.einsum(
        "ksjgi,sikh->ksjgh", w_new.astype(jnp.bfloat16), fresh_v, preferred_element_type=jnp.float32
    )
    lead = (kv_local, SAMPLE_COUNT, DECODE_TOKENS, query_groups)
    source_out = jnp.transpose(source_out.reshape((HEAD_SIZE,) + lead), (1, 2, 3, 4, 0))
    source_top = source_top.reshape(lead)
    source_sum = source_sum.reshape(lead)
    overall = jnp.maximum(source_top, local_top)
    source_w = jnp.exp(source_top - overall)
    local_w = jnp.exp(local_top - overall)
    numer = source_w[..., None] * source_out + local_w[..., None] * local_out
    denom = source_w * source_sum + local_w * local_sum
    attention_layer = (numer / denom[..., None]).astype(jnp.bfloat16)
    attention_layer = jnp.transpose(attention_layer, (1, 2, 0, 3, 4)).reshape(
        SAMPLE_COUNT * DECODE_TOKENS, kv_local * query_groups * HEAD_SIZE
    )
    projected = jnp.dot(attention_layer, out_weight, preferred_element_type=jnp.float32)
    mlp_index = lax.axis_index("mlp")
    share = D // mlp_count
    mid = residual_in.astype(jnp.float32) + sum_all(projected, "mlp", mlp_count)
    normed = (mid * rms_scale(jnp.sum(mid * mid, -1, keepdims=True), D) * mlp_gain).astype(
        jnp.bfloat16
    )
    gate = jnp.dot(normed, gate_weight, preferred_element_type=jnp.float32)
    upper = jnp.dot(normed, up_weight, preferred_element_type=jnp.float32)
    hidden = (jax.nn.silu(gate) * upper).astype(jnp.bfloat16)
    stream = mid + sum_all(
        jnp.dot(hidden, down_weight, preferred_element_type=jnp.float32), "mlp", mlp_count
    )
    score = jnp.sum(
        stream
        * rms_scale(jnp.sum(stream * stream, -1, keepdims=True), D)
        * final_gain
        * score_weight,
        -1,
    )
    layer_out = lax.dynamic_slice_in_dim(stream, mlp_index * share, share, 1).astype(jnp.bfloat16)
    return (layer_out, score)


def solution(mesh):
    placed = (
        P("req", None),
        P("req", "mlp"),
        P("req", "mlp"),
        P("req", "mlp"),
        P(None, "req", "mlp"),
        P(None, "req", "mlp"),
        P("req", None, None, "mlp"),
        P("req", None, None, "mlp"),
        P(),
        P("req", None),
        P("mlp", None),
        P(None, "mlp"),
        P(None, "mlp"),
        P("mlp", None),
        P(),
        P(),
        P(),
    )
    return jax.shard_map(
        on_device,
        mesh=mesh,
        in_specs=placed,
        out_specs=(P("req", "mlp"), P("req")),
        check_vma=False,
    )
```

```python
import jax
import jax.numpy as jnp
from jax import lax
from jax.experimental import pallas as pl
from jax.experimental.pallas import tpu as pltpu
from jax.sharding import PartitionSpec as P

D = 2560
QUERY_HEADS = 32
KEY_VALUE_HEADS = 8
HEAD_SIZE = 80
SAMPLE_COUNT = 16
DECODE_TOKENS = 2
TAIL_LENGTH = 128


PACK = 88

def prefix_kernel(count_ref, q_ref, k_ref, v_ref, out_ref):
    p = pl.program_id(0)
    q = q_ref[0]
    k = k_ref[0]
    v = v_ref[0]
    s = lax.dot_general(k, q, (((1,), (1,)), ((), ())), preferred_element_type=jnp.float32)
    s = s * (HEAD_SIZE ** -0.5)
    place = lax.broadcasted_iota(jnp.int32, s.shape, 0)
    valid = place < count_ref[p]
    s = jnp.where(valid, s, jnp.float32(-1e30))
    top = jnp.max(s, axis=0, keepdims=True)
    w = jnp.where(valid, jnp.exp(s - top), 0.0)
    total = jnp.sum(w, axis=0, keepdims=True)
    o = lax.dot_general(v, w.astype(jnp.bfloat16), (((0,), (0,)), ((), ())), preferred_element_type=jnp.float32)
    out_ref[0, 0:HEAD_SIZE, :] = o
    out_ref[0, HEAD_SIZE:HEAD_SIZE + 1, :] = top
    out_ref[0, HEAD_SIZE + 1:HEAD_SIZE + 2, :] = total
    out_ref[0, HEAD_SIZE + 2:PACK, :] = jnp.zeros((PACK - HEAD_SIZE - 2, s.shape[1]), jnp.float32)

def prefix_partials(count, q, k, v):
    P_, rows, _ = q.shape
    L = k.shape[1]
    return pl.pallas_call(
        prefix_kernel,
        grid_spec=pltpu.PrefetchScalarGridSpec(
            num_scalar_prefetch=1,
            grid=(P_,),
            in_specs=[
                pl.BlockSpec((1, rows, HEAD_SIZE), lambda p, c: (p, 0, 0)),
                pl.BlockSpec((1, L, HEAD_SIZE), lambda p, c: (p, 0, 0)),
                pl.BlockSpec((1, L, HEAD_SIZE), lambda p, c: (p, 0, 0)),
            ],
            out_specs=pl.BlockSpec((1, PACK, rows), lambda p, c: (p, 0, 0)),
        ),
        out_shape=jax.ShapeDtypeStruct((P_, PACK, rows), jnp.float32),
        cost_estimate=pl.CostEstimate(flops=4 * P_ * rows * L * HEAD_SIZE, transcendentals=P_ * rows * L,
                                      bytes_accessed=2 * P_ * L * HEAD_SIZE * 2 + P_ * rows * HEAD_SIZE * 2 + P_ * PACK * rows * 4),
    )(count, q, k, v)

def rms_scale(total_sq, width):
    return lax.rsqrt(total_sq / width + 1e-05)


def exchange(x, axis, n, bit):
    return lax.ppermute(x, axis, perm=[(i, i ^ (1 << bit)) for i in range(n)])


def gather_rows(x, axis, n, bits):
    me = lax.axis_index(axis)
    buf = x[None]
    taken = []
    for b in bits:
        other = exchange(buf, axis, n, b)
        high = ((me >> b) & 1) == 1
        buf = jnp.stack([jnp.where(high, other, buf), jnp.where(high, buf, other)])
        taken.insert(0, b)
    nb = len(bits)
    order = sorted(range(nb), key=lambda i: -taken[i])
    buf = jnp.transpose(buf, order + list(range(nb, buf.ndim)))
    return buf.reshape((n * x.shape[0],) + x.shape[1:])


def merge_partials(a, b):
    ma = a[..., HEAD_SIZE:HEAD_SIZE + 1, :]
    mb = b[..., HEAD_SIZE:HEAD_SIZE + 1, :]
    top = jnp.maximum(ma, mb)
    wa = jnp.exp(ma - top)
    wb = jnp.exp(mb - top)
    outs = a[..., :HEAD_SIZE, :] * wa + b[..., :HEAD_SIZE, :] * wb
    sums = a[..., HEAD_SIZE + 1:, :] * wa + b[..., HEAD_SIZE + 1:, :] * wb
    return jnp.concatenate([outs, top, sums], axis=-2)


def reduce_partials(packed, axis, n, bits):
    me = lax.axis_index(axis)
    nb = len(bits)
    cur = packed.reshape((2,) * nb + packed.shape[1:])
    left = list(range(nb - 1, -1, -1))
    for b in bits:
        ax = left.index(b)
        own = (me >> b) & 1
        keep = lax.dynamic_index_in_dim(cur, own, ax, keepdims=False)
        send = lax.dynamic_index_in_dim(cur, 1 - own, ax, keepdims=False)
        cur = merge_partials(keep, exchange(send, axis, n, b))
        left.remove(b)
    return cur


def allreduce_bf16(x, axis, n, bits):
    cur = x.astype(jnp.bfloat16)
    for b in bits:
        other = exchange(cur, axis, n, b)
        cur = (cur.astype(jnp.float32) + other.astype(jnp.float32)).astype(jnp.bfloat16)
    return cur


def on_device(
    residual_in,
    queries,
    fresh_rotated_keys,
    fresh_value_rows,
    shared_prefix_keys,
    shared_prefix_values,
    sample_tail_keys,
    sample_tail_values,
    prompt_prefix_length,
    sample_tail_length,
    out_weight,
    gate_weight,
    up_weight,
    down_weight,
    mlp_gain,
    final_gain,
    score_weight,
):
    query_groups = QUERY_HEADS // KEY_VALUE_HEADS
    inv_root = HEAD_SIZE ** (-0.5)
    kv_local = fresh_rotated_keys.shape[1] // HEAD_SIZE
    prompts = shared_prefix_keys.shape[0]
    piece_len = shared_prefix_keys.shape[1]
    req_count = lax.axis_size("req")
    req_bits = req_count.bit_length() - 1
    mlp_count = lax.axis_size("mlp")
    mlp_bits = mlp_count.bit_length() - 1
    req_index = lax.axis_index("req")
    low = jnp.float32(-1e30)
    rows = kv_local * SAMPLE_COUNT * DECODE_TOKENS * query_groups

    gather_order = [req_bits - 1] + ([1] if req_bits > 1 else []) + list(range(req_bits - 2, 1, -1)) + [0]
    gather_order = [b for i, b in enumerate(gather_order) if b not in gather_order[:i]]
    reduce_order = gather_order[::-1]

    gathered = gather_rows(queries, "req", req_count, gather_order)
    query_all = gathered.reshape(prompts, rows, HEAD_SIZE)
    prefix_key_block = shared_prefix_keys.reshape(prompts, piece_len, HEAD_SIZE * kv_local)
    prefix_value_block = shared_prefix_values.reshape(prompts, piece_len, HEAD_SIZE * kv_local)
    count = jnp.clip(prompt_prefix_length - req_index * piece_len, 0, piece_len).astype(jnp.int32)
    packed = prefix_partials(count, query_all, prefix_key_block, prefix_value_block)
    own_part = reduce_partials(packed, "req", req_count, reduce_order)

    query_own = queries.reshape(SAMPLE_COUNT, DECODE_TOKENS, kv_local, query_groups, HEAD_SIZE)
    tail_key_block = sample_tail_keys.reshape(SAMPLE_COUNT, TAIL_LENGTH, kv_local, HEAD_SIZE)
    tail_value_block = sample_tail_values.reshape(SAMPLE_COUNT, TAIL_LENGTH, kv_local, HEAD_SIZE)
    fresh_k = fresh_rotated_keys.reshape(SAMPLE_COUNT, DECODE_TOKENS, kv_local, HEAD_SIZE)
    fresh_v = fresh_value_rows.reshape(SAMPLE_COUNT, DECODE_TOKENS, kv_local, HEAD_SIZE)
    score_tail = (
        jnp.einsum(
            "sjkgh,stkh->ksjgt", query_own, tail_key_block, preferred_element_type=jnp.float32
        )
        * inv_root
    )
    score_new = (
        jnp.einsum("sjkgh,sikh->ksjgi", query_own, fresh_k, preferred_element_type=jnp.float32)
        * inv_root
    )
    mask_tail = (jnp.arange(TAIL_LENGTH)[None, :] < sample_tail_length[0][:, None])[
        None, :, None, None, :
    ]
    causal = (jnp.arange(DECODE_TOKENS)[None, :] <= jnp.arange(DECODE_TOKENS)[:, None])[
        None, None, :, None, :
    ]
    local_top = jnp.maximum(
        jnp.max(jnp.where(mask_tail, score_tail, low), -1),
        jnp.max(jnp.where(causal, score_new, low), -1),
    )
    w_tail = jnp.where(mask_tail, jnp.exp(score_tail - local_top[..., None]), 0.0)
    w_new = jnp.where(causal, jnp.exp(score_new - local_top[..., None]), 0.0)
    local_sum = jnp.sum(w_tail, -1) + jnp.sum(w_new, -1)
    local_out = jnp.einsum(
        "ksjgt,stkh->ksjgh",
        w_tail.astype(jnp.bfloat16),
        tail_value_block,
        preferred_element_type=jnp.float32,
    )
    local_out = local_out + jnp.einsum(
        "ksjgi,sikh->ksjgh", w_new.astype(jnp.bfloat16), fresh_v, preferred_element_type=jnp.float32
    )
    lead = (kv_local, SAMPLE_COUNT, DECODE_TOKENS, query_groups)
    source_out = jnp.transpose(own_part[:HEAD_SIZE].reshape((HEAD_SIZE,) + lead), (1, 2, 3, 4, 0))
    source_top = own_part[HEAD_SIZE].reshape(lead)
    source_sum = own_part[HEAD_SIZE + 1].reshape(lead)
    overall = jnp.maximum(source_top, local_top)
    source_w = jnp.exp(source_top - overall)
    local_w = jnp.exp(local_top - overall)
    numer = source_w[..., None] * source_out + local_w[..., None] * local_out
    denom = source_w * source_sum + local_w * local_sum
    attention_layer = (numer / denom[..., None]).astype(jnp.bfloat16)
    attention_layer = jnp.transpose(attention_layer, (1, 2, 0, 3, 4)).reshape(
        SAMPLE_COUNT * DECODE_TOKENS, kv_local * query_groups * HEAD_SIZE
    )
    projected = jnp.dot(attention_layer, out_weight, preferred_element_type=jnp.float32)
    mlp_index = lax.axis_index("mlp")
    share = D // mlp_count
    mlp_order = list(range(mlp_bits - 1, -1, -1))
    mid = residual_in.astype(jnp.float32) + allreduce_bf16(
        projected, "mlp", mlp_count, mlp_order
    ).astype(jnp.float32)
    normed = (mid * rms_scale(jnp.sum(mid * mid, -1, keepdims=True), D) * mlp_gain).astype(
        jnp.bfloat16
    )
    gate = jnp.dot(normed, gate_weight, preferred_element_type=jnp.float32)
    upper = jnp.dot(normed, up_weight, preferred_element_type=jnp.float32)
    hidden = (jax.nn.silu(gate) * upper).astype(jnp.bfloat16)
    stream = mid + allreduce_bf16(
        jnp.dot(hidden, down_weight, preferred_element_type=jnp.float32), "mlp", mlp_count, mlp_order
    ).astype(jnp.float32)
    score = jnp.sum(
        stream
        * rms_scale(jnp.sum(stream * stream, -1, keepdims=True), D)
        * final_gain
        * score_weight,
        -1,
    )
    layer_out = lax.dynamic_slice_in_dim(stream, mlp_index * share, share, 1).astype(jnp.bfloat16)
    return (layer_out, score)


def solution(mesh):
    placed = (
        P("req", None),
        P("req", "mlp"),
        P("req", "mlp"),
        P("req", "mlp"),
        P(None, "req", "mlp"),
        P(None, "req", "mlp"),
        P("req", None, None, "mlp"),
        P("req", None, None, "mlp"),
        P(),
        P("req", None),
        P("mlp", None),
        P(None, "mlp"),
        P(None, "mlp"),
        P("mlp", None),
        P(),
        P(),
        P(),
    )
    return jax.shard_map(
        on_device,
        mesh=mesh,
        in_specs=placed,
        out_specs=(P("req", "mlp"), P("req")),
        check_vma=False,
    )
```

```python
import jax
import jax.numpy as jnp
from jax import lax
from jax.experimental import pallas as pl
from jax.experimental.pallas import tpu as pltpu
from jax.sharding import PartitionSpec as P

D = 2560
QUERY_HEADS = 32
KEY_VALUE_HEADS = 8
HEAD_SIZE = 80
SAMPLE_COUNT = 16
DECODE_TOKENS = 2
TAIL_LENGTH = 128


PACK = 88
BLOCK_PROMPTS = 4


def prefix_kernel(count_ref, q_ref, kt_ref, vt_ref, out_ref):
    step = pl.program_id(0)
    for i in range(q_ref.shape[0]):
        q = q_ref[i]
        kt = kt_ref[i]
        vt = vt_ref[i]
        s = jnp.dot(q, kt, preferred_element_type=jnp.float32) * (HEAD_SIZE ** -0.5)
        place = lax.broadcasted_iota(jnp.int32, s.shape, 1)
        valid = place < count_ref[step * q_ref.shape[0] + i]
        s = jnp.where(valid, s, jnp.float32(-1e30))
        top = jnp.max(s, axis=1, keepdims=True)
        w = jnp.where(valid, jnp.exp(s - top), 0.0)
        total = jnp.sum(w, axis=1, keepdims=True)
        o = lax.dot_general(vt, w.astype(jnp.bfloat16), (((1,), (1,)), ((), ())),
                            preferred_element_type=jnp.float32)
        lane = lax.broadcasted_iota(jnp.int32, (s.shape[0], 128), 1)
        stats = jnp.where(lane == 0, top, jnp.where(lane == 1, total, 0.0))
        out_ref[i, 0:HEAD_SIZE, :] = o
        out_ref[i, HEAD_SIZE:PACK, :] = jnp.transpose(stats)[0:PACK - HEAD_SIZE, :]


def prefix_partials(count, q, kt, vt):
    P_, rows, _ = q.shape
    L = kt.shape[2]
    bp = BLOCK_PROMPTS
    return pl.pallas_call(
        prefix_kernel,
        grid_spec=pltpu.PrefetchScalarGridSpec(
            num_scalar_prefetch=1,
            grid=(P_ // bp,),
            in_specs=[
                pl.BlockSpec((bp, rows, HEAD_SIZE), lambda p, c: (p, 0, 0)),
                pl.BlockSpec((bp, HEAD_SIZE, L), lambda p, c: (p, 0, 0)),
                pl.BlockSpec((bp, HEAD_SIZE, L), lambda p, c: (p, 0, 0)),
            ],
            out_specs=pl.BlockSpec((bp, PACK, rows), lambda p, c: (p, 0, 0)),
        ),
        out_shape=jax.ShapeDtypeStruct((P_, PACK, rows), jnp.float32),
        cost_estimate=pl.CostEstimate(flops=4 * P_ * rows * L * HEAD_SIZE, transcendentals=P_ * rows * L,
                                      bytes_accessed=2 * P_ * L * HEAD_SIZE * 2 + P_ * rows * HEAD_SIZE * 2 + P_ * PACK * rows * 4),
    )(count, q, kt, vt)


def rms_scale(total_sq, width):
    return lax.rsqrt(total_sq / width + 1e-05)


def exchange(x, axis, n, bit):
    return lax.ppermute(x, axis, perm=[(i, i ^ (1 << bit)) for i in range(n)])


def gather_rows(x, axis, n, bits):
    me = lax.axis_index(axis)
    buf = x[None]
    taken = []
    for b in bits:
        other = exchange(buf, axis, n, b)
        high = ((me >> b) & 1) == 1
        buf = jnp.stack([jnp.where(high, other, buf), jnp.where(high, buf, other)])
        taken.insert(0, b)
    nb = len(bits)
    order = sorted(range(nb), key=lambda i: -taken[i])
    buf = jnp.transpose(buf, order + list(range(nb, buf.ndim)))
    return buf.reshape((n * x.shape[0],) + x.shape[1:])


def merge_partials(a, b):
    ma = a[..., HEAD_SIZE:HEAD_SIZE + 1, :]
    mb = b[..., HEAD_SIZE:HEAD_SIZE + 1, :]
    top = jnp.maximum(ma, mb)
    wa = jnp.exp(ma - top)
    wb = jnp.exp(mb - top)
    outs = a[..., :HEAD_SIZE, :] * wa + b[..., :HEAD_SIZE, :] * wb
    sums = a[..., HEAD_SIZE + 1:, :] * wa + b[..., HEAD_SIZE + 1:, :] * wb
    return jnp.concatenate([outs, top, sums], axis=-2)


def reduce_partials(packed, axis, n, bits):
    me = lax.axis_index(axis)
    nb = len(bits)
    cur = packed.reshape((2,) * nb + packed.shape[1:])
    left = list(range(nb - 1, -1, -1))
    for b in bits:
        ax = left.index(b)
        own = (me >> b) & 1
        keep = lax.dynamic_index_in_dim(cur, own, ax, keepdims=False)
        send = lax.dynamic_index_in_dim(cur, 1 - own, ax, keepdims=False)
        cur = merge_partials(keep, exchange(send, axis, n, b))
        left.remove(b)
    return cur


def allreduce_bf16(x, axis, n, bits):
    cur = x.astype(jnp.bfloat16)
    for b in bits:
        other = exchange(cur, axis, n, b)
        cur = (cur.astype(jnp.float32) + other.astype(jnp.float32)).astype(jnp.bfloat16)
    return cur


def on_device(
    residual_in,
    queries,
    fresh_rotated_keys,
    fresh_value_rows,
    shared_prefix_keys,
    shared_prefix_values,
    sample_tail_keys,
    sample_tail_values,
    prompt_prefix_length,
    sample_tail_length,
    out_weight,
    gate_weight,
    up_weight,
    down_weight,
    mlp_gain,
    final_gain,
    score_weight,
):
    query_groups = QUERY_HEADS // KEY_VALUE_HEADS
    inv_root = HEAD_SIZE ** (-0.5)
    kv_local = fresh_rotated_keys.shape[1] // HEAD_SIZE
    prompts = shared_prefix_keys.shape[0]
    piece_len = shared_prefix_keys.shape[1]
    req_count = lax.axis_size("req")
    req_bits = req_count.bit_length() - 1
    mlp_count = lax.axis_size("mlp")
    mlp_bits = mlp_count.bit_length() - 1
    req_index = lax.axis_index("req")
    low = jnp.float32(-1e30)
    rows = kv_local * SAMPLE_COUNT * DECODE_TOKENS * query_groups

    gather_order = [req_bits - 1] + ([1] if req_bits > 1 else []) + list(range(req_bits - 2, 1, -1)) + [0]
    gather_order = [b for i, b in enumerate(gather_order) if b not in gather_order[:i]]
    reduce_order = gather_order[::-1]

    gathered = gather_rows(queries, "req", req_count, gather_order)
    query_all = gathered.reshape(prompts, rows, HEAD_SIZE)
    prefix_key_block = jnp.swapaxes(shared_prefix_keys.reshape(prompts, piece_len, HEAD_SIZE * kv_local), 1, 2)
    prefix_value_block = jnp.swapaxes(shared_prefix_values.reshape(prompts, piece_len, HEAD_SIZE * kv_local), 1, 2)
    count = jnp.clip(prompt_prefix_length - req_index * piece_len, 0, piece_len).astype(jnp.int32)
    packed = prefix_partials(count, query_all, prefix_key_block, prefix_value_block)
    own_part = reduce_partials(packed, "req", req_count, reduce_order)

    query_own = queries.reshape(SAMPLE_COUNT, DECODE_TOKENS, kv_local, query_groups, HEAD_SIZE)
    tail_key_block = sample_tail_keys.reshape(SAMPLE_COUNT, TAIL_LENGTH, kv_local, HEAD_SIZE)
    tail_value_block = sample_tail_values.reshape(SAMPLE_COUNT, TAIL_LENGTH, kv_local, HEAD_SIZE)
    fresh_k = fresh_rotated_keys.reshape(SAMPLE_COUNT, DECODE_TOKENS, kv_local, HEAD_SIZE)
    fresh_v = fresh_value_rows.reshape(SAMPLE_COUNT, DECODE_TOKENS, kv_local, HEAD_SIZE)
    score_tail = (
        jnp.einsum(
            "sjkgh,stkh->ksjgt", query_own, tail_key_block, preferred_element_type=jnp.float32
        )
        * inv_root
    )
    score_new = (
        jnp.einsum("sjkgh,sikh->ksjgi", query_own, fresh_k, preferred_element_type=jnp.float32)
        * inv_root
    )
    mask_tail = (jnp.arange(TAIL_LENGTH)[None, :] < sample_tail_length[0][:, None])[
        None, :, None, None, :
    ]
    causal = (jnp.arange(DECODE_TOKENS)[None, :] <= jnp.arange(DECODE_TOKENS)[:, None])[
        None, None, :, None, :
    ]
    local_top = jnp.maximum(
        jnp.max(jnp.where(mask_tail, score_tail, low), -1),
        jnp.max(jnp.where(causal, score_new, low), -1),
    )
    w_tail = jnp.where(mask_tail, jnp.exp(score_tail - local_top[..., None]), 0.0)
    w_new = jnp.where(causal, jnp.exp(score_new - local_top[..., None]), 0.0)
    local_sum = jnp.sum(w_tail, -1) + jnp.sum(w_new, -1)
    local_out = jnp.einsum(
        "ksjgt,stkh->ksjgh",
        w_tail.astype(jnp.bfloat16),
        tail_value_block,
        preferred_element_type=jnp.float32,
    )
    local_out = local_out + jnp.einsum(
        "ksjgi,sikh->ksjgh", w_new.astype(jnp.bfloat16), fresh_v, preferred_element_type=jnp.float32
    )
    lead = (kv_local, SAMPLE_COUNT, DECODE_TOKENS, query_groups)
    source_out = jnp.transpose(own_part[:HEAD_SIZE].reshape((HEAD_SIZE,) + lead), (1, 2, 3, 4, 0))
    source_top = own_part[HEAD_SIZE].reshape(lead)
    source_sum = own_part[HEAD_SIZE + 1].reshape(lead)
    overall = jnp.maximum(source_top, local_top)
    source_w = jnp.exp(source_top - overall)
    local_w = jnp.exp(local_top - overall)
    numer = source_w[..., None] * source_out + local_w[..., None] * local_out
    denom = source_w * source_sum + local_w * local_sum
    attention_layer = (numer / denom[..., None]).astype(jnp.bfloat16)
    attention_layer = jnp.transpose(attention_layer, (1, 2, 0, 3, 4)).reshape(
        SAMPLE_COUNT * DECODE_TOKENS, kv_local * query_groups * HEAD_SIZE
    )
    projected = jnp.dot(attention_layer, out_weight, preferred_element_type=jnp.float32)
    mlp_index = lax.axis_index("mlp")
    share = D // mlp_count
    mlp_order = list(range(mlp_bits - 1, -1, -1))
    mid = residual_in.astype(jnp.float32) + allreduce_bf16(
        projected, "mlp", mlp_count, mlp_order
    ).astype(jnp.float32)
    normed = (mid * rms_scale(jnp.sum(mid * mid, -1, keepdims=True), D) * mlp_gain).astype(
        jnp.bfloat16
    )
    gate = jnp.dot(normed, gate_weight, preferred_element_type=jnp.float32)
    upper = jnp.dot(normed, up_weight, preferred_element_type=jnp.float32)
    hidden = (jax.nn.silu(gate) * upper).astype(jnp.bfloat16)
    stream = mid + allreduce_bf16(
        jnp.dot(hidden, down_weight, preferred_element_type=jnp.float32), "mlp", mlp_count, mlp_order
    ).astype(jnp.float32)
    score = jnp.sum(
        stream
        * rms_scale(jnp.sum(stream * stream, -1, keepdims=True), D)
        * final_gain
        * score_weight,
        -1,
    )
    layer_out = lax.dynamic_slice_in_dim(stream, mlp_index * share, share, 1).astype(jnp.bfloat16)
    return (layer_out, score)


def solution(mesh):
    placed = (
        P("req", None),
        P("req", "mlp"),
        P("req", "mlp"),
        P("req", "mlp"),
        P(None, "req", "mlp"),
        P(None, "req", "mlp"),
        P("req", None, None, "mlp"),
        P("req", None, None, "mlp"),
        P(),
        P("req", None),
        P("mlp", None),
        P(None, "mlp"),
        P(None, "mlp"),
        P("mlp", None),
        P(),
        P(),
        P(),
    )
    return jax.shard_map(
        on_device,
        mesh=mesh,
        in_specs=placed,
        out_specs=(P("req", "mlp"), P("req")),
        check_vma=False,
    )
```

```python
import jax
import jax.numpy as jnp
from jax import lax
from jax.experimental import pallas as pl
from jax.experimental.pallas import tpu as pltpu
from jax.sharding import PartitionSpec as P

D = 2560
QUERY_HEADS = 32
KEY_VALUE_HEADS = 8
HEAD_SIZE = 80
SAMPLE_COUNT = 16
DECODE_TOKENS = 2
TAIL_LENGTH = 128


PACK = 88
BLOCK_PROMPTS = 4


def prefix_kernel(count_ref, q_ref, kt_ref, vt_ref, out_ref):
    step = pl.program_id(0)
    for i in range(q_ref.shape[0]):
        q = q_ref[i]
        kt = kt_ref[i]
        vt = vt_ref[i]
        s = jnp.dot(q, kt, preferred_element_type=jnp.float32) * (HEAD_SIZE ** -0.5)
        place = lax.broadcasted_iota(jnp.int32, s.shape, 1)
        valid = place < count_ref[step * q_ref.shape[0] + i]
        s = jnp.where(valid, s, jnp.float32(-1e30))
        top = jnp.max(s, axis=1, keepdims=True)
        w = jnp.where(valid, jnp.exp(s - top), 0.0)
        total = jnp.sum(w, axis=1, keepdims=True)
        o = lax.dot_general(vt, w.astype(jnp.bfloat16), (((1,), (1,)), ((), ())),
                            preferred_element_type=jnp.float32)
        lane = lax.broadcasted_iota(jnp.int32, (s.shape[0], 128), 1)
        stats = jnp.where(lane == 0, top, jnp.where(lane == 1, total, 0.0))
        out_ref[i, 0:HEAD_SIZE, :] = o
        out_ref[i, HEAD_SIZE:PACK, :] = jnp.transpose(stats)[0:PACK - HEAD_SIZE, :]


def prefix_partials(count, q, kt, vt):
    P_, rows, _ = q.shape
    L = kt.shape[2]
    bp = BLOCK_PROMPTS
    return pl.pallas_call(
        prefix_kernel,
        grid_spec=pltpu.PrefetchScalarGridSpec(
            num_scalar_prefetch=1,
            grid=(P_ // bp,),
            in_specs=[
                pl.BlockSpec((bp, rows, HEAD_SIZE), lambda p, c: (p, 0, 0)),
                pl.BlockSpec((bp, HEAD_SIZE, L), lambda p, c: (p, 0, 0)),
                pl.BlockSpec((bp, HEAD_SIZE, L), lambda p, c: (p, 0, 0)),
            ],
            out_specs=pl.BlockSpec((bp, PACK, rows), lambda p, c: (p, 0, 0)),
        ),
        out_shape=jax.ShapeDtypeStruct((P_, PACK, rows), jnp.float32),
        cost_estimate=pl.CostEstimate(flops=4 * P_ * rows * L * HEAD_SIZE, transcendentals=P_ * rows * L,
                                      bytes_accessed=2 * P_ * L * HEAD_SIZE * 2 + P_ * rows * HEAD_SIZE * 2 + P_ * PACK * rows * 4),
    )(count, q, kt, vt)


def rms_scale(total_sq, width):
    return lax.rsqrt(total_sq / width + 1e-05)


def exchange(x, axis, n, bit):
    return lax.ppermute(x, axis, perm=[(i, i ^ (1 << bit)) for i in range(n)])


def gather_rows(x, axis, n, bits):
    me = lax.axis_index(axis)
    buf = x[None]
    taken = []
    for b in bits:
        other = exchange(buf, axis, n, b)
        high = ((me >> b) & 1) == 1
        buf = jnp.stack([jnp.where(high, other, buf), jnp.where(high, buf, other)])
        taken.insert(0, b)
    nb = len(bits)
    order = sorted(range(nb), key=lambda i: -taken[i])
    buf = jnp.transpose(buf, order + list(range(nb, buf.ndim)))
    return buf.reshape((n * x.shape[0],) + x.shape[1:])


def merge_partials(a, b):
    ma = a[..., HEAD_SIZE:HEAD_SIZE + 1, :]
    mb = b[..., HEAD_SIZE:HEAD_SIZE + 1, :]
    top = jnp.maximum(ma, mb)
    wa = jnp.exp(ma - top)
    wb = jnp.exp(mb - top)
    outs = a[..., :HEAD_SIZE, :] * wa + b[..., :HEAD_SIZE, :] * wb
    sums = a[..., HEAD_SIZE + 1:, :] * wa + b[..., HEAD_SIZE + 1:, :] * wb
    return jnp.concatenate([outs, top, sums], axis=-2)


def encode_partials(x):
    stats = x[..., HEAD_SIZE:HEAD_SIZE + 2, :]
    hi = lax.reduce_precision(stats, exponent_bits=8, mantissa_bits=7)
    rest = stats - hi
    mid = lax.reduce_precision(rest, exponent_bits=8, mantissa_bits=7)
    lo = rest - mid
    pad = jnp.zeros(x.shape[:-2] + (PACK - HEAD_SIZE - 6, x.shape[-1]), jnp.float32)
    return jnp.concatenate([x[..., :HEAD_SIZE, :], hi, mid, lo, pad], axis=-2).astype(jnp.bfloat16)


def decode_partials(y):
    y = y.astype(jnp.float32)
    base = HEAD_SIZE
    stats = (y[..., base:base + 2, :] + y[..., base + 2:base + 4, :]) + y[..., base + 4:base + 6, :]
    pad = jnp.zeros(y.shape[:-2] + (PACK - HEAD_SIZE - 2, y.shape[-1]), jnp.float32)
    return jnp.concatenate([y[..., :HEAD_SIZE, :], stats, pad], axis=-2)


def reduce_partials(packed, axis, n, bits):
    me = lax.axis_index(axis)
    nb = len(bits)
    cur = packed.reshape((2,) * nb + packed.shape[1:])
    left = list(range(nb - 1, -1, -1))
    for i, b in enumerate(bits):
        ax = left.index(b)
        own = (me >> b) & 1
        keep = lax.dynamic_index_in_dim(cur, own, ax, keepdims=False)
        send = lax.dynamic_index_in_dim(cur, 1 - own, ax, keepdims=False)
        if i == 0:
            got = exchange(send, axis, n, b)
        else:
            got = decode_partials(exchange(encode_partials(send), axis, n, b))
        cur = merge_partials(keep, got)
        left.remove(b)
    return cur


def allreduce_bf16(x, axis, n, bits):
    cur = x.astype(jnp.bfloat16)
    for b in bits:
        other = exchange(cur, axis, n, b)
        cur = (cur.astype(jnp.float32) + other.astype(jnp.float32)).astype(jnp.bfloat16)
    return cur


def on_device(
    residual_in,
    queries,
    fresh_rotated_keys,
    fresh_value_rows,
    shared_prefix_keys,
    shared_prefix_values,
    sample_tail_keys,
    sample_tail_values,
    prompt_prefix_length,
    sample_tail_length,
    out_weight,
    gate_weight,
    up_weight,
    down_weight,
    mlp_gain,
    final_gain,
    score_weight,
):
    query_groups = QUERY_HEADS // KEY_VALUE_HEADS
    inv_root = HEAD_SIZE ** (-0.5)
    kv_local = fresh_rotated_keys.shape[1] // HEAD_SIZE
    prompts = shared_prefix_keys.shape[0]
    piece_len = shared_prefix_keys.shape[1]
    req_count = lax.axis_size("req")
    req_bits = req_count.bit_length() - 1
    mlp_count = lax.axis_size("mlp")
    mlp_bits = mlp_count.bit_length() - 1
    req_index = lax.axis_index("req")
    low = jnp.float32(-1e30)
    rows = kv_local * SAMPLE_COUNT * DECODE_TOKENS * query_groups

    gather_order = [req_bits - 1] + ([1] if req_bits > 1 else []) + list(range(req_bits - 2, 1, -1)) + [0]
    gather_order = [b for i, b in enumerate(gather_order) if b not in gather_order[:i]]
    reduce_order = gather_order[::-1]

    gathered = gather_rows(queries, "req", req_count, gather_order)
    query_all = gathered.reshape(prompts, rows, HEAD_SIZE)
    prefix_key_block = jnp.swapaxes(shared_prefix_keys.reshape(prompts, piece_len, HEAD_SIZE * kv_local), 1, 2)
    prefix_value_block = jnp.swapaxes(shared_prefix_values.reshape(prompts, piece_len, HEAD_SIZE * kv_local), 1, 2)
    count = jnp.clip(prompt_prefix_length - req_index * piece_len, 0, piece_len).astype(jnp.int32)
    packed = prefix_partials(count, query_all, prefix_key_block, prefix_value_block)
    own_part = reduce_partials(packed, "req", req_count, reduce_order)

    query_own = queries.reshape(SAMPLE_COUNT, DECODE_TOKENS, kv_local, query_groups, HEAD_SIZE)
    tail_key_block = sample_tail_keys.reshape(SAMPLE_COUNT, TAIL_LENGTH, kv_local, HEAD_SIZE)
    tail_value_block = sample_tail_values.reshape(SAMPLE_COUNT, TAIL_LENGTH, kv_local, HEAD_SIZE)
    fresh_k = fresh_rotated_keys.reshape(SAMPLE_COUNT, DECODE_TOKENS, kv_local, HEAD_SIZE)
    fresh_v = fresh_value_rows.reshape(SAMPLE_COUNT, DECODE_TOKENS, kv_local, HEAD_SIZE)
    score_tail = (
        jnp.einsum(
            "sjkgh,stkh->ksjgt", query_own, tail_key_block, preferred_element_type=jnp.float32
        )
        * inv_root
    )
    score_new = (
        jnp.einsum("sjkgh,sikh->ksjgi", query_own, fresh_k, preferred_element_type=jnp.float32)
        * inv_root
    )
    mask_tail = (jnp.arange(TAIL_LENGTH)[None, :] < sample_tail_length[0][:, None])[
        None, :, None, None, :
    ]
    causal = (jnp.arange(DECODE_TOKENS)[None, :] <= jnp.arange(DECODE_TOKENS)[:, None])[
        None, None, :, None, :
    ]
    local_top = jnp.maximum(
        jnp.max(jnp.where(mask_tail, score_tail, low), -1),
        jnp.max(jnp.where(causal, score_new, low), -1),
    )
    w_tail = jnp.where(mask_tail, jnp.exp(score_tail - local_top[..., None]), 0.0)
    w_new = jnp.where(causal, jnp.exp(score_new - local_top[..., None]), 0.0)
    local_sum = jnp.sum(w_tail, -1) + jnp.sum(w_new, -1)
    local_out = jnp.einsum(
        "ksjgt,stkh->ksjgh",
        w_tail.astype(jnp.bfloat16),
        tail_value_block,
        preferred_element_type=jnp.float32,
    )
    local_out = local_out + jnp.einsum(
        "ksjgi,sikh->ksjgh", w_new.astype(jnp.bfloat16), fresh_v, preferred_element_type=jnp.float32
    )
    lead = (kv_local, SAMPLE_COUNT, DECODE_TOKENS, query_groups)
    source_out = jnp.transpose(own_part[:HEAD_SIZE].reshape((HEAD_SIZE,) + lead), (1, 2, 3, 4, 0))
    source_top = own_part[HEAD_SIZE].reshape(lead)
    source_sum = own_part[HEAD_SIZE + 1].reshape(lead)
    overall = jnp.maximum(source_top, local_top)
    source_w = jnp.exp(source_top - overall)
    local_w = jnp.exp(local_top - overall)
    numer = source_w[..., None] * source_out + local_w[..., None] * local_out
    denom = source_w * source_sum + local_w * local_sum
    attention_layer = (numer / denom[..., None]).astype(jnp.bfloat16)
    attention_layer = jnp.transpose(attention_layer, (1, 2, 0, 3, 4)).reshape(
        SAMPLE_COUNT * DECODE_TOKENS, kv_local * query_groups * HEAD_SIZE
    )
    projected = jnp.dot(attention_layer, out_weight, preferred_element_type=jnp.float32)
    mlp_index = lax.axis_index("mlp")
    share = D // mlp_count
    mlp_order = list(range(mlp_bits - 1, -1, -1))
    mid = residual_in.astype(jnp.float32) + allreduce_bf16(
        projected, "mlp", mlp_count, mlp_order
    ).astype(jnp.float32)
    normed = (mid * rms_scale(jnp.sum(mid * mid, -1, keepdims=True), D) * mlp_gain).astype(
        jnp.bfloat16
    )
    gate = jnp.dot(normed, gate_weight, preferred_element_type=jnp.float32)
    upper = jnp.dot(normed, up_weight, preferred_element_type=jnp.float32)
    hidden = (jax.nn.silu(gate) * upper).astype(jnp.bfloat16)
    stream = mid + allreduce_bf16(
        jnp.dot(hidden, down_weight, preferred_element_type=jnp.float32), "mlp", mlp_count, mlp_order
    ).astype(jnp.float32)
    score = jnp.sum(
        stream
        * rms_scale(jnp.sum(stream * stream, -1, keepdims=True), D)
        * final_gain
        * score_weight,
        -1,
    )
    layer_out = lax.dynamic_slice_in_dim(stream, mlp_index * share, share, 1).astype(jnp.bfloat16)
    return (layer_out, score)


def solution(mesh):
    placed = (
        P("req", None),
        P("req", "mlp"),
        P("req", "mlp"),
        P("req", "mlp"),
        P(None, "req", "mlp"),
        P(None, "req", "mlp"),
        P("req", None, None, "mlp"),
        P("req", None, None, "mlp"),
        P(),
        P("req", None),
        P("mlp", None),
        P(None, "mlp"),
        P(None, "mlp"),
        P("mlp", None),
        P(),
        P(),
        P(),
    )
    return jax.shard_map(
        on_device,
        mesh=mesh,
        in_specs=placed,
        out_specs=(P("req", "mlp"), P("req")),
        check_vma=False,
    )
```

```python
import jax
import jax.numpy as jnp
from jax import lax
from jax.experimental import pallas as pl
from jax.experimental.pallas import tpu as pltpu
from jax.sharding import PartitionSpec as P

D = 2560
QUERY_HEADS = 32
KEY_VALUE_HEADS = 8
HEAD_SIZE = 80
SAMPLE_COUNT = 16
DECODE_TOKENS = 2
TAIL_LENGTH = 128


PACK = 88
BLOCK_PROMPTS = 8


def prefix_kernel(count_ref, half_ref, q_ref, kt_ref, vt_ref, out_ref):
    step = pl.program_id(0)
    for i in range(q_ref.shape[0]):
        q = q_ref[i]
        kt = kt_ref[i]
        vt = vt_ref[i]
        s = jnp.dot(q, kt, preferred_element_type=jnp.float32) * (HEAD_SIZE ** -0.5)
        place = lax.broadcasted_iota(jnp.int32, s.shape, 1)
        valid = place < count_ref[2 * (step * q_ref.shape[0] + i) + half_ref[0]]
        s = jnp.where(valid, s, jnp.float32(-1e30))
        top = jnp.max(s, axis=1, keepdims=True)
        w = jnp.where(valid, jnp.exp(s - top), 0.0)
        total = jnp.sum(w, axis=1, keepdims=True)
        o = lax.dot_general(vt, w.astype(jnp.bfloat16), (((1,), (1,)), ((), ())),
                            preferred_element_type=jnp.float32)
        lane = lax.broadcasted_iota(jnp.int32, (s.shape[0], 128), 1)
        stats = jnp.where(lane == 0, top, jnp.where(lane == 1, total, 0.0))
        out_ref[i, 0:HEAD_SIZE, :] = o
        out_ref[i, HEAD_SIZE:PACK, :] = jnp.transpose(stats)[0:PACK - HEAD_SIZE, :]


def prefix_partials(count, half, q, kt, vt):
    pairs, _, rows, _ = q.shape
    L = kt.shape[3]
    bp = min(BLOCK_PROMPTS, pairs)
    return pl.pallas_call(
        prefix_kernel,
        grid_spec=pltpu.PrefetchScalarGridSpec(
            num_scalar_prefetch=2,
            grid=(pairs // bp,),
            in_specs=[
                pl.BlockSpec((bp, None, rows, HEAD_SIZE), lambda p, c, h: (p, h[0], 0, 0)),
                pl.BlockSpec((bp, None, HEAD_SIZE, L), lambda p, c, h: (p, h[0], 0, 0)),
                pl.BlockSpec((bp, None, HEAD_SIZE, L), lambda p, c, h: (p, h[0], 0, 0)),
            ],
            out_specs=pl.BlockSpec((bp, PACK, rows), lambda p, c, h: (p, 0, 0)),
        ),
        out_shape=jax.ShapeDtypeStruct((pairs, PACK, rows), jnp.float32),
        cost_estimate=pl.CostEstimate(flops=4 * pairs * rows * L * HEAD_SIZE, transcendentals=pairs * rows * L,
                                      bytes_accessed=2 * pairs * L * HEAD_SIZE * 2 + pairs * rows * HEAD_SIZE * 2 + pairs * PACK * rows * 4),
    )(count, half, q, kt, vt)


def rms_scale(total_sq, width):
    return lax.rsqrt(total_sq / width + 1e-05)


def exchange(x, axis, n, bit):
    return lax.ppermute(x, axis, perm=[(i, i ^ (1 << bit)) for i in range(n)])


def gather_rows(x, axis, n, bits):
    me = lax.axis_index(axis)
    buf = x[None]
    taken = []
    for b in bits:
        other = exchange(buf, axis, n, b)
        high = ((me >> b) & 1) == 1
        buf = jnp.stack([jnp.where(high, other, buf), jnp.where(high, buf, other)])
        taken.insert(0, b)
    nb = len(bits)
    order = sorted(range(nb), key=lambda i: -taken[i])
    buf = jnp.transpose(buf, order + list(range(nb, buf.ndim)))
    return buf.reshape((n * x.shape[0],) + x.shape[1:])


def merge_partials(a, b):
    ma = a[..., HEAD_SIZE:HEAD_SIZE + 1, :]
    mb = b[..., HEAD_SIZE:HEAD_SIZE + 1, :]
    top = jnp.maximum(ma, mb)
    wa = jnp.exp(ma - top)
    wb = jnp.exp(mb - top)
    outs = a[..., :HEAD_SIZE, :] * wa + b[..., :HEAD_SIZE, :] * wb
    sums = a[..., HEAD_SIZE + 1:, :] * wa + b[..., HEAD_SIZE + 1:, :] * wb
    return jnp.concatenate([outs, top, sums], axis=-2)


def encode_partials(x):
    stats = x[..., HEAD_SIZE:HEAD_SIZE + 2, :]
    hi = lax.reduce_precision(stats, exponent_bits=8, mantissa_bits=7)
    rest = stats - hi
    mid = lax.reduce_precision(rest, exponent_bits=8, mantissa_bits=7)
    lo = rest - mid
    pad = jnp.zeros(x.shape[:-2] + (PACK - HEAD_SIZE - 6, x.shape[-1]), jnp.float32)
    return jnp.concatenate([x[..., :HEAD_SIZE, :], hi, mid, lo, pad], axis=-2).astype(jnp.bfloat16)


def decode_partials(y):
    y = y.astype(jnp.float32)
    base = HEAD_SIZE
    stats = (y[..., base:base + 2, :] + y[..., base + 2:base + 4, :]) + y[..., base + 4:base + 6, :]
    pad = jnp.zeros(y.shape[:-2] + (PACK - HEAD_SIZE - 2, y.shape[-1]), jnp.float32)
    return jnp.concatenate([y[..., :HEAD_SIZE, :], stats, pad], axis=-2)


def reduce_partials(cur, axis, n, left, bits):
    me = lax.axis_index(axis)
    left = list(left)
    for b in bits:
        ax = left.index(b)
        own = (me >> b) & 1
        keep = lax.dynamic_index_in_dim(cur, own, ax, keepdims=False)
        send = lax.dynamic_index_in_dim(cur, 1 - own, ax, keepdims=False)
        got = decode_partials(exchange(encode_partials(send), axis, n, b))
        cur = merge_partials(keep, got)
        left.remove(b)
    return cur


def allreduce_bf16(x, axis, n, bits):
    cur = x.astype(jnp.bfloat16)
    for b in bits:
        other = exchange(cur, axis, n, b)
        cur = (cur.astype(jnp.float32) + other.astype(jnp.float32)).astype(jnp.bfloat16)
    return cur


def on_device(
    residual_in,
    queries,
    fresh_rotated_keys,
    fresh_value_rows,
    shared_prefix_keys,
    shared_prefix_values,
    sample_tail_keys,
    sample_tail_values,
    prompt_prefix_length,
    sample_tail_length,
    out_weight,
    gate_weight,
    up_weight,
    down_weight,
    mlp_gain,
    final_gain,
    score_weight,
):
    query_groups = QUERY_HEADS // KEY_VALUE_HEADS
    inv_root = HEAD_SIZE ** (-0.5)
    kv_local = fresh_rotated_keys.shape[1] // HEAD_SIZE
    prompts = shared_prefix_keys.shape[0]
    piece_len = shared_prefix_keys.shape[1]
    req_count = lax.axis_size("req")
    req_bits = req_count.bit_length() - 1
    mlp_count = lax.axis_size("mlp")
    mlp_bits = mlp_count.bit_length() - 1
    req_index = lax.axis_index("req")
    low = jnp.float32(-1e30)
    rows = kv_local * SAMPLE_COUNT * DECODE_TOKENS * query_groups

    gather_order = [req_bits - 1] + ([1] if req_bits > 1 else []) + list(range(req_bits - 2, 1, -1)) + [0]
    gather_order = [b for i, b in enumerate(gather_order) if b not in gather_order[:i]]
    reduce_order = gather_order[::-1]

    gathered = gather_rows(queries, "req", req_count, gather_order)
    pairs = prompts // 2
    query_all = gathered.reshape(pairs, 2, rows, HEAD_SIZE)
    prefix_key_block = jnp.swapaxes(
        shared_prefix_keys.reshape(pairs, 2, piece_len, HEAD_SIZE * kv_local), 2, 3
    )
    prefix_value_block = jnp.swapaxes(
        shared_prefix_values.reshape(pairs, 2, piece_len, HEAD_SIZE * kv_local), 2, 3
    )
    count = jnp.clip(prompt_prefix_length - req_index * piece_len, 0, piece_len).astype(jnp.int32)
    own_low = (req_index & 1).astype(jnp.int32)
    send_half = prefix_partials(
        count, (1 - own_low)[None], query_all, prefix_key_block, prefix_value_block
    )
    got = exchange(send_half, "req", req_count, 0)
    keep_half = prefix_partials(count, own_low[None], query_all, prefix_key_block, prefix_value_block)
    merged = merge_partials(keep_half, got)
    nb = req_count.bit_length() - 1
    merged = merged.reshape((2,) * (nb - 1) + merged.shape[1:])
    own_part = reduce_partials(
        merged, "req", req_count, list(range(nb - 1, 0, -1)), [b for b in reduce_order if b != 0]
    )

    query_own = queries.reshape(SAMPLE_COUNT, DECODE_TOKENS, kv_local, query_groups, HEAD_SIZE)
    tail_key_block = sample_tail_keys.reshape(SAMPLE_COUNT, TAIL_LENGTH, kv_local, HEAD_SIZE)
    tail_value_block = sample_tail_values.reshape(SAMPLE_COUNT, TAIL_LENGTH, kv_local, HEAD_SIZE)
    fresh_k = fresh_rotated_keys.reshape(SAMPLE_COUNT, DECODE_TOKENS, kv_local, HEAD_SIZE)
    fresh_v = fresh_value_rows.reshape(SAMPLE_COUNT, DECODE_TOKENS, kv_local, HEAD_SIZE)
    score_tail = (
        jnp.einsum(
            "sjkgh,stkh->ksjgt", query_own, tail_key_block, preferred_element_type=jnp.float32
        )
        * inv_root
    )
    score_new = (
        jnp.einsum("sjkgh,sikh->ksjgi", query_own, fresh_k, preferred_element_type=jnp.float32)
        * inv_root
    )
    mask_tail = (jnp.arange(TAIL_LENGTH)[None, :] < sample_tail_length[0][:, None])[
        None, :, None, None, :
    ]
    causal = (jnp.arange(DECODE_TOKENS)[None, :] <= jnp.arange(DECODE_TOKENS)[:, None])[
        None, None, :, None, :
    ]
    local_top = jnp.maximum(
        jnp.max(jnp.where(mask_tail, score_tail, low), -1),
        jnp.max(jnp.where(causal, score_new, low), -1),
    )
    w_tail = jnp.where(mask_tail, jnp.exp(score_tail - local_top[..., None]), 0.0)
    w_new = jnp.where(causal, jnp.exp(score_new - local_top[..., None]), 0.0)
    local_sum = jnp.sum(w_tail, -1) + jnp.sum(w_new, -1)
    local_out = jnp.einsum(
        "ksjgt,stkh->ksjgh",
        w_tail.astype(jnp.bfloat16),
        tail_value_block,
        preferred_element_type=jnp.float32,
    )
    local_out = local_out + jnp.einsum(
        "ksjgi,sikh->ksjgh", w_new.astype(jnp.bfloat16), fresh_v, preferred_element_type=jnp.float32
    )
    lead = (kv_local, SAMPLE_COUNT, DECODE_TOKENS, query_groups)
    source_out = jnp.transpose(own_part[:HEAD_SIZE].reshape((HEAD_SIZE,) + lead), (1, 2, 3, 4, 0))
    source_top = own_part[HEAD_SIZE].reshape(lead)
    source_sum = own_part[HEAD_SIZE + 1].reshape(lead)
    overall = jnp.maximum(source_top, local_top)
    source_w = jnp.exp(source_top - overall)
    local_w = jnp.exp(local_top - overall)
    numer = source_w[..., None] * source_out + local_w[..., None] * local_out
    denom = source_w * source_sum + local_w * local_sum
    attention_layer = (numer / denom[..., None]).astype(jnp.bfloat16)
    attention_layer = jnp.transpose(attention_layer, (1, 2, 0, 3, 4)).reshape(
        SAMPLE_COUNT * DECODE_TOKENS, kv_local * query_groups * HEAD_SIZE
    )
    projected = jnp.dot(attention_layer, out_weight, preferred_element_type=jnp.float32)
    mlp_index = lax.axis_index("mlp")
    share = D // mlp_count
    mlp_order = list(range(mlp_bits - 1, -1, -1))
    mid = residual_in.astype(jnp.float32) + allreduce_bf16(
        projected, "mlp", mlp_count, mlp_order
    ).astype(jnp.float32)
    normed = (mid * rms_scale(jnp.sum(mid * mid, -1, keepdims=True), D) * mlp_gain).astype(
        jnp.bfloat16
    )
    gate = jnp.dot(normed, gate_weight, preferred_element_type=jnp.float32)
    upper = jnp.dot(normed, up_weight, preferred_element_type=jnp.float32)
    hidden = (jax.nn.silu(gate) * upper).astype(jnp.bfloat16)
    stream = mid + allreduce_bf16(
        jnp.dot(hidden, down_weight, preferred_element_type=jnp.float32), "mlp", mlp_count, mlp_order
    ).astype(jnp.float32)
    score = jnp.sum(
        stream
        * rms_scale(jnp.sum(stream * stream, -1, keepdims=True), D)
        * final_gain
        * score_weight,
        -1,
    )
    layer_out = lax.dynamic_slice_in_dim(stream, mlp_index * share, share, 1).astype(jnp.bfloat16)
    return (layer_out, score)


def solution(mesh):
    placed = (
        P("req", None),
        P("req", "mlp"),
        P("req", "mlp"),
        P("req", "mlp"),
        P(None, "req", "mlp"),
        P(None, "req", "mlp"),
        P("req", None, None, "mlp"),
        P("req", None, None, "mlp"),
        P(),
        P("req", None),
        P("mlp", None),
        P(None, "mlp"),
        P(None, "mlp"),
        P("mlp", None),
        P(),
        P(),
        P(),
    )
    return jax.shard_map(
        on_device,
        mesh=mesh,
        in_specs=placed,
        out_specs=(P("req", "mlp"), P("req")),
        check_vma=False,
    )
```

```python
import jax
import jax.numpy as jnp
from jax import lax
from jax.experimental import pallas as pl
from jax.experimental.pallas import tpu as pltpu
from jax.sharding import PartitionSpec as P

D = 2560
QUERY_HEADS = 32
KEY_VALUE_HEADS = 8
HEAD_SIZE = 80
SAMPLE_COUNT = 16
DECODE_TOKENS = 2
TAIL_LENGTH = 128


PACK = 88
BLOCK_PROMPTS = 8


def prefix_kernel(count_ref, half_ref, q_ref, kt_ref, vt_ref, out_ref):
    step = pl.program_id(0)
    for i in range(q_ref.shape[0]):
        q = q_ref[i]
        kt = kt_ref[i]
        vt = vt_ref[i]
        s = jnp.dot(q, kt, preferred_element_type=jnp.float32) * (HEAD_SIZE ** -0.5)
        place = lax.broadcasted_iota(jnp.int32, s.shape, 1)
        valid = place < count_ref[2 * (step * q_ref.shape[0] + i) + half_ref[0]]
        s = jnp.where(valid, s, jnp.float32(-1e30))
        top = jnp.max(s, axis=1, keepdims=True)
        w = jnp.where(valid, jnp.exp(s - top), 0.0)
        total = jnp.sum(w, axis=1, keepdims=True)
        o = lax.dot_general(vt, w.astype(jnp.bfloat16), (((1,), (1,)), ((), ())),
                            preferred_element_type=jnp.float32)
        lane = lax.broadcasted_iota(jnp.int32, (s.shape[0], 128), 1)
        stats = jnp.where(lane == 0, top, jnp.where(lane == 1, total, 0.0))
        out_ref[i, 0:HEAD_SIZE, :] = o
        out_ref[i, HEAD_SIZE:PACK, :] = jnp.transpose(stats)[0:PACK - HEAD_SIZE, :]


def prefix_partials(count, half, q, kt, vt):
    pairs, _, rows, _ = q.shape
    L = kt.shape[3]
    bp = min(BLOCK_PROMPTS, pairs)
    return pl.pallas_call(
        prefix_kernel,
        grid_spec=pltpu.PrefetchScalarGridSpec(
            num_scalar_prefetch=2,
            grid=(pairs // bp,),
            in_specs=[
                pl.BlockSpec((bp, None, rows, HEAD_SIZE), lambda p, c, h: (p, h[0], 0, 0)),
                pl.BlockSpec((bp, None, HEAD_SIZE, L), lambda p, c, h: (p, h[0], 0, 0)),
                pl.BlockSpec((bp, None, HEAD_SIZE, L), lambda p, c, h: (p, h[0], 0, 0)),
            ],
            out_specs=pl.BlockSpec((bp, PACK, rows), lambda p, c, h: (p, 0, 0)),
        ),
        out_shape=jax.ShapeDtypeStruct((pairs, PACK, rows), jnp.float32),
        cost_estimate=pl.CostEstimate(flops=4 * pairs * rows * L * HEAD_SIZE, transcendentals=pairs * rows * L,
                                      bytes_accessed=2 * pairs * L * HEAD_SIZE * 2 + pairs * rows * HEAD_SIZE * 2 + pairs * PACK * rows * 4),
    )(count, half, q, kt, vt)


def rms_scale(total_sq, width):
    return lax.rsqrt(total_sq / width + 1e-05)


def exchange(x, axis, n, bit):
    return lax.ppermute(x, axis, perm=[(i, i ^ (1 << bit)) for i in range(n)])


def gather_rows(x, axis, n, bits):
    me = lax.axis_index(axis)
    buf = x[None]
    taken = []
    for b in bits:
        other = exchange(buf, axis, n, b)
        high = ((me >> b) & 1) == 1
        buf = jnp.stack([jnp.where(high, other, buf), jnp.where(high, buf, other)])
        taken.insert(0, b)
    nb = len(bits)
    order = sorted(range(nb), key=lambda i: -taken[i])
    buf = jnp.transpose(buf, order + list(range(nb, buf.ndim)))
    return buf.reshape((n * x.shape[0],) + x.shape[1:])


def merge_partials(a, b):
    ma = a[..., HEAD_SIZE:HEAD_SIZE + 1, :]
    mb = b[..., HEAD_SIZE:HEAD_SIZE + 1, :]
    top = jnp.maximum(ma, mb)
    wa = jnp.exp(ma - top)
    wb = jnp.exp(mb - top)
    outs = a[..., :HEAD_SIZE, :] * wa + b[..., :HEAD_SIZE, :] * wb
    sums = a[..., HEAD_SIZE + 1:, :] * wa + b[..., HEAD_SIZE + 1:, :] * wb
    return jnp.concatenate([outs, top, sums], axis=-2)


def encode_partials(x):
    stats = x[..., HEAD_SIZE:HEAD_SIZE + 2, :]
    hi = lax.reduce_precision(stats, exponent_bits=8, mantissa_bits=7)
    rest = stats - hi
    mid = lax.reduce_precision(rest, exponent_bits=8, mantissa_bits=7)
    lo = rest - mid
    pad = jnp.zeros(x.shape[:-2] + (PACK - HEAD_SIZE - 6, x.shape[-1]), jnp.float32)
    return jnp.concatenate([x[..., :HEAD_SIZE, :], hi, mid, lo, pad], axis=-2).astype(jnp.bfloat16)


def decode_partials(y):
    y = y.astype(jnp.float32)
    base = HEAD_SIZE
    stats = (y[..., base:base + 2, :] + y[..., base + 2:base + 4, :]) + y[..., base + 4:base + 6, :]
    pad = jnp.zeros(y.shape[:-2] + (PACK - HEAD_SIZE - 2, y.shape[-1]), jnp.float32)
    return jnp.concatenate([y[..., :HEAD_SIZE, :], stats, pad], axis=-2)


def reduce_partials(cur, axis, n, left, bits):
    me = lax.axis_index(axis)
    left = list(left)
    for b in bits:
        ax = left.index(b)
        own = (me >> b) & 1
        keep = lax.dynamic_index_in_dim(cur, own, ax, keepdims=False)
        send = lax.dynamic_index_in_dim(cur, 1 - own, ax, keepdims=False)
        got = decode_partials(exchange(encode_partials(send), axis, n, b))
        cur = merge_partials(keep, got)
        left.remove(b)
    return cur


def allreduce_bf16(x, axis, n, masks):
    cur = x.astype(jnp.bfloat16)
    for m in masks:
        other = lax.ppermute(cur, axis, perm=[(i, i ^ m) for i in range(n)])
        cur = (cur.astype(jnp.float32) + other.astype(jnp.float32)).astype(jnp.bfloat16)
    return cur


def on_device(
    residual_in,
    queries,
    fresh_rotated_keys,
    fresh_value_rows,
    shared_prefix_keys,
    shared_prefix_values,
    sample_tail_keys,
    sample_tail_values,
    prompt_prefix_length,
    sample_tail_length,
    out_weight,
    gate_weight,
    up_weight,
    down_weight,
    mlp_gain,
    final_gain,
    score_weight,
):
    query_groups = QUERY_HEADS // KEY_VALUE_HEADS
    inv_root = HEAD_SIZE ** (-0.5)
    kv_local = fresh_rotated_keys.shape[1] // HEAD_SIZE
    prompts = shared_prefix_keys.shape[0]
    piece_len = shared_prefix_keys.shape[1]
    req_count = lax.axis_size("req")
    req_bits = req_count.bit_length() - 1
    mlp_count = lax.axis_size("mlp")
    mlp_bits = mlp_count.bit_length() - 1
    req_index = lax.axis_index("req")
    low = jnp.float32(-1e30)
    rows = kv_local * SAMPLE_COUNT * DECODE_TOKENS * query_groups

    gather_order = [req_bits - 1] + ([1] if req_bits > 1 else []) + list(range(req_bits - 2, 1, -1)) + [0]
    gather_order = [b for i, b in enumerate(gather_order) if b not in gather_order[:i]]
    reduce_order = gather_order[::-1]

    gathered = gather_rows(queries, "req", req_count, gather_order)
    pairs = prompts // 2
    query_all = gathered.reshape(pairs, 2, rows, HEAD_SIZE)
    prefix_key_block = jnp.swapaxes(
        shared_prefix_keys.reshape(pairs, 2, piece_len, HEAD_SIZE * kv_local), 2, 3
    )
    prefix_value_block = jnp.swapaxes(
        shared_prefix_values.reshape(pairs, 2, piece_len, HEAD_SIZE * kv_local), 2, 3
    )
    count = jnp.clip(prompt_prefix_length - req_index * piece_len, 0, piece_len).astype(jnp.int32)
    own_low = (req_index & 1).astype(jnp.int32)
    send_half = prefix_partials(
        count, (1 - own_low)[None], query_all, prefix_key_block, prefix_value_block
    )
    got = exchange(send_half, "req", req_count, 0)
    keep_half = prefix_partials(count, own_low[None], query_all, prefix_key_block, prefix_value_block)
    merged = merge_partials(keep_half, got)
    nb = req_count.bit_length() - 1
    merged = merged.reshape((2,) * (nb - 1) + merged.shape[1:])
    own_part = reduce_partials(
        merged, "req", req_count, list(range(nb - 1, 0, -1)), [b for b in reduce_order if b != 0]
    )

    query_own = queries.reshape(SAMPLE_COUNT, DECODE_TOKENS, kv_local, query_groups, HEAD_SIZE)
    tail_key_block = sample_tail_keys.reshape(SAMPLE_COUNT, TAIL_LENGTH, kv_local, HEAD_SIZE)
    tail_value_block = sample_tail_values.reshape(SAMPLE_COUNT, TAIL_LENGTH, kv_local, HEAD_SIZE)
    fresh_k = fresh_rotated_keys.reshape(SAMPLE_COUNT, DECODE_TOKENS, kv_local, HEAD_SIZE)
    fresh_v = fresh_value_rows.reshape(SAMPLE_COUNT, DECODE_TOKENS, kv_local, HEAD_SIZE)
    score_tail = (
        jnp.einsum(
            "sjkgh,stkh->ksjgt", query_own, tail_key_block, preferred_element_type=jnp.float32
        )
        * inv_root
    )
    score_new = (
        jnp.einsum("sjkgh,sikh->ksjgi", query_own, fresh_k, preferred_element_type=jnp.float32)
        * inv_root
    )
    mask_tail = (jnp.arange(TAIL_LENGTH)[None, :] < sample_tail_length[0][:, None])[
        None, :, None, None, :
    ]
    causal = (jnp.arange(DECODE_TOKENS)[None, :] <= jnp.arange(DECODE_TOKENS)[:, None])[
        None, None, :, None, :
    ]
    local_top = jnp.maximum(
        jnp.max(jnp.where(mask_tail, score_tail, low), -1),
        jnp.max(jnp.where(causal, score_new, low), -1),
    )
    w_tail = jnp.where(mask_tail, jnp.exp(score_tail - local_top[..., None]), 0.0)
    w_new = jnp.where(causal, jnp.exp(score_new - local_top[..., None]), 0.0)
    local_sum = jnp.sum(w_tail, -1) + jnp.sum(w_new, -1)
    local_out = jnp.einsum(
        "ksjgt,stkh->ksjgh",
        w_tail.astype(jnp.bfloat16),
        tail_value_block,
        preferred_element_type=jnp.float32,
    )
    local_out = local_out + jnp.einsum(
        "ksjgi,sikh->ksjgh", w_new.astype(jnp.bfloat16), fresh_v, preferred_element_type=jnp.float32
    )
    lead = (kv_local, SAMPLE_COUNT, DECODE_TOKENS, query_groups)
    source_out = jnp.transpose(own_part[:HEAD_SIZE].reshape((HEAD_SIZE,) + lead), (1, 2, 3, 4, 0))
    source_top = own_part[HEAD_SIZE].reshape(lead)
    source_sum = own_part[HEAD_SIZE + 1].reshape(lead)
    overall = jnp.maximum(source_top, local_top)
    source_w = jnp.exp(source_top - overall)
    local_w = jnp.exp(local_top - overall)
    numer = source_w[..., None] * source_out + local_w[..., None] * local_out
    denom = source_w * source_sum + local_w * local_sum
    attention_layer = (numer / denom[..., None]).astype(jnp.bfloat16)
    attention_layer = jnp.transpose(attention_layer, (1, 2, 0, 3, 4)).reshape(
        SAMPLE_COUNT * DECODE_TOKENS, kv_local * query_groups * HEAD_SIZE
    )
    projected = jnp.dot(attention_layer, out_weight, preferred_element_type=jnp.float32)
    mlp_index = lax.axis_index("mlp")
    share = D // mlp_count
    mlp_order = [4, 1, 3] if mlp_count == 8 else [1 << b for b in range(mlp_bits)]
    mid = residual_in.astype(jnp.float32) + allreduce_bf16(
        projected, "mlp", mlp_count, mlp_order
    ).astype(jnp.float32)
    normed = (mid * rms_scale(jnp.sum(mid * mid, -1, keepdims=True), D) * mlp_gain).astype(
        jnp.bfloat16
    )
    gate = jnp.dot(normed, gate_weight, preferred_element_type=jnp.float32)
    upper = jnp.dot(normed, up_weight, preferred_element_type=jnp.float32)
    hidden = (jax.nn.silu(gate) * upper).astype(jnp.bfloat16)
    stream = mid + allreduce_bf16(
        jnp.dot(hidden, down_weight, preferred_element_type=jnp.float32), "mlp", mlp_count, mlp_order
    ).astype(jnp.float32)
    score = jnp.sum(
        stream
        * rms_scale(jnp.sum(stream * stream, -1, keepdims=True), D)
        * final_gain
        * score_weight,
        -1,
    )
    layer_out = lax.dynamic_slice_in_dim(stream, mlp_index * share, share, 1).astype(jnp.bfloat16)
    return (layer_out, score)


def solution(mesh):
    placed = (
        P("req", None),
        P("req", "mlp"),
        P("req", "mlp"),
        P("req", "mlp"),
        P(None, "req", "mlp"),
        P(None, "req", "mlp"),
        P("req", None, None, "mlp"),
        P("req", None, None, "mlp"),
        P(),
        P("req", None),
        P("mlp", None),
        P(None, "mlp"),
        P(None, "mlp"),
        P("mlp", None),
        P(),
        P(),
        P(),
    )
    return jax.shard_map(
        on_device,
        mesh=mesh,
        in_specs=placed,
        out_specs=(P("req", "mlp"), P("req")),
        check_vma=False,
    )
```

```python
import jax
import jax.numpy as jnp
from jax import lax
from jax.experimental import pallas as pl
from jax.experimental.pallas import tpu as pltpu
from jax.sharding import PartitionSpec as P

D = 2560
QUERY_HEADS = 32
KEY_VALUE_HEADS = 8
HEAD_SIZE = 80
SAMPLE_COUNT = 16
DECODE_TOKENS = 2
TAIL_LENGTH = 128


PACK = 88
BLOCK_PROMPTS = 8


def prefix_kernel(count_ref, half_ref, q_ref, kt_ref, vt_ref, out_ref):
    step = pl.program_id(0)
    for i in range(q_ref.shape[0]):
        q = q_ref[i]
        kt = kt_ref[i]
        vt = vt_ref[i]
        s = jnp.dot(q, kt, preferred_element_type=jnp.float32) * (HEAD_SIZE ** -0.5)
        place = lax.broadcasted_iota(jnp.int32, s.shape, 1)
        valid = place < count_ref[2 * (step * q_ref.shape[0] + i) + half_ref[0]]
        s = jnp.where(valid, s, jnp.float32(-1e30))
        top = jnp.max(s, axis=1, keepdims=True)
        w = jnp.where(valid, jnp.exp(s - top), 0.0)
        total = jnp.sum(w, axis=1, keepdims=True)
        o = lax.dot_general(vt, w.astype(jnp.bfloat16), (((1,), (1,)), ((), ())),
                            preferred_element_type=jnp.float32)
        lane = lax.broadcasted_iota(jnp.int32, (s.shape[0], 128), 1)
        stats = jnp.where(lane == 0, top, jnp.where(lane == 1, total, 0.0))
        out_ref[i, 0:HEAD_SIZE, :] = o
        out_ref[i, HEAD_SIZE:PACK, :] = jnp.transpose(stats)[0:PACK - HEAD_SIZE, :]


def prefix_partials(count, half, q, kt, vt):
    pairs, _, rows, _ = q.shape
    L = kt.shape[3]
    bp = min(BLOCK_PROMPTS, pairs)
    return pl.pallas_call(
        prefix_kernel,
        grid_spec=pltpu.PrefetchScalarGridSpec(
            num_scalar_prefetch=2,
            grid=(pairs // bp,),
            in_specs=[
                pl.BlockSpec((bp, None, rows, HEAD_SIZE), lambda p, c, h: (p, h[0], 0, 0)),
                pl.BlockSpec((bp, None, HEAD_SIZE, L), lambda p, c, h: (p, h[0], 0, 0)),
                pl.BlockSpec((bp, None, HEAD_SIZE, L), lambda p, c, h: (p, h[0], 0, 0)),
            ],
            out_specs=pl.BlockSpec((bp, PACK, rows), lambda p, c, h: (p, 0, 0)),
        ),
        out_shape=jax.ShapeDtypeStruct((pairs, PACK, rows), jnp.float32),
        cost_estimate=pl.CostEstimate(flops=4 * pairs * rows * L * HEAD_SIZE, transcendentals=pairs * rows * L,
                                      bytes_accessed=2 * pairs * L * HEAD_SIZE * 2 + pairs * rows * HEAD_SIZE * 2 + pairs * PACK * rows * 4),
    )(count, half, q, kt, vt)


def rms_scale(total_sq, width):
    return lax.rsqrt(total_sq / width + 1e-05)


def exchange(x, axis, n, bit):
    return lax.ppermute(x, axis, perm=[(i, i ^ (1 << bit)) for i in range(n)])


def gather_rows(x, axis, n, bits):
    me = lax.axis_index(axis)
    buf = x[None]
    taken = []
    for b in bits:
        other = exchange(buf, axis, n, b)
        high = ((me >> b) & 1) == 1
        buf = jnp.stack([jnp.where(high, other, buf), jnp.where(high, buf, other)])
        taken.insert(0, b)
    nb = len(bits)
    order = sorted(range(nb), key=lambda i: -taken[i])
    buf = jnp.transpose(buf, order + list(range(nb, buf.ndim)))
    return buf.reshape((n * x.shape[0],) + x.shape[1:])


def merge_partials(a, b):
    ma = a[..., HEAD_SIZE:HEAD_SIZE + 1, :]
    mb = b[..., HEAD_SIZE:HEAD_SIZE + 1, :]
    top = jnp.maximum(ma, mb)
    wa = jnp.exp(ma - top)
    wb = jnp.exp(mb - top)
    outs = a[..., :HEAD_SIZE, :] * wa + b[..., :HEAD_SIZE, :] * wb
    sums = a[..., HEAD_SIZE + 1:, :] * wa + b[..., HEAD_SIZE + 1:, :] * wb
    return jnp.concatenate([outs, top, sums], axis=-2)


def encode_partials(x):
    stats = x[..., HEAD_SIZE:HEAD_SIZE + 2, :]
    hi = lax.reduce_precision(stats, exponent_bits=8, mantissa_bits=7)
    rest = stats - hi
    mid = lax.reduce_precision(rest, exponent_bits=8, mantissa_bits=7)
    lo = rest - mid
    pad = jnp.zeros(x.shape[:-2] + (PACK - HEAD_SIZE - 6, x.shape[-1]), jnp.float32)
    return jnp.concatenate([x[..., :HEAD_SIZE, :], hi, mid, lo, pad], axis=-2).astype(jnp.bfloat16)


def decode_partials(y):
    y = y.astype(jnp.float32)
    base = HEAD_SIZE
    stats = (y[..., base:base + 2, :] + y[..., base + 2:base + 4, :]) + y[..., base + 4:base + 6, :]
    pad = jnp.zeros(y.shape[:-2] + (PACK - HEAD_SIZE - 2, y.shape[-1]), jnp.float32)
    return jnp.concatenate([y[..., :HEAD_SIZE, :], stats, pad], axis=-2)


def reduce_partials(cur, axis, n, left, bits):
    me = lax.axis_index(axis)
    left = list(left)
    for b in bits:
        ax = left.index(b)
        own = (me >> b) & 1
        keep = lax.dynamic_index_in_dim(cur, own, ax, keepdims=False)
        send = lax.dynamic_index_in_dim(cur, 1 - own, ax, keepdims=False)
        got = decode_partials(exchange(encode_partials(send), axis, n, b))
        cur = merge_partials(keep, got)
        left.remove(b)
    return cur


def allreduce_bf16(x, req_count, mlp_count, orders):
    cur = x.astype(jnp.bfloat16)
    for k in range(len(orders[0])):
        perm = []
        for r in range(req_count):
            mask = orders[r % len(orders)][k]
            perm += [(r * mlp_count + m, r * mlp_count + (m ^ mask)) for m in range(mlp_count)]
        other = lax.ppermute(cur, ("req", "mlp"), perm=perm)
        cur = (cur.astype(jnp.float32) + other.astype(jnp.float32)).astype(jnp.bfloat16)
    return cur


def on_device(
    residual_in,
    queries,
    fresh_rotated_keys,
    fresh_value_rows,
    shared_prefix_keys,
    shared_prefix_values,
    sample_tail_keys,
    sample_tail_values,
    prompt_prefix_length,
    sample_tail_length,
    out_weight,
    gate_weight,
    up_weight,
    down_weight,
    mlp_gain,
    final_gain,
    score_weight,
):
    query_groups = QUERY_HEADS // KEY_VALUE_HEADS
    inv_root = HEAD_SIZE ** (-0.5)
    kv_local = fresh_rotated_keys.shape[1] // HEAD_SIZE
    prompts = shared_prefix_keys.shape[0]
    piece_len = shared_prefix_keys.shape[1]
    req_count = lax.axis_size("req")
    req_bits = req_count.bit_length() - 1
    mlp_count = lax.axis_size("mlp")
    mlp_bits = mlp_count.bit_length() - 1
    req_index = lax.axis_index("req")
    low = jnp.float32(-1e30)
    rows = kv_local * SAMPLE_COUNT * DECODE_TOKENS * query_groups

    gather_order = [req_bits - 1] + ([1] if req_bits > 1 else []) + list(range(req_bits - 2, 1, -1)) + [0]
    gather_order = [b for i, b in enumerate(gather_order) if b not in gather_order[:i]]
    reduce_order = gather_order[::-1]

    gathered = gather_rows(queries, "req", req_count, gather_order)
    pairs = prompts // 2
    query_all = gathered.reshape(pairs, 2, rows, HEAD_SIZE)
    prefix_key_block = jnp.swapaxes(
        shared_prefix_keys.reshape(pairs, 2, piece_len, HEAD_SIZE * kv_local), 2, 3
    )
    prefix_value_block = jnp.swapaxes(
        shared_prefix_values.reshape(pairs, 2, piece_len, HEAD_SIZE * kv_local), 2, 3
    )
    count = jnp.clip(prompt_prefix_length - req_index * piece_len, 0, piece_len).astype(jnp.int32)
    own_low = (req_index & 1).astype(jnp.int32)
    send_half = prefix_partials(
        count, (1 - own_low)[None], query_all, prefix_key_block, prefix_value_block
    )
    got = exchange(send_half, "req", req_count, 0)
    keep_half = prefix_partials(count, own_low[None], query_all, prefix_key_block, prefix_value_block)
    merged = merge_partials(keep_half, got)
    nb = req_count.bit_length() - 1
    merged = merged.reshape((2,) * (nb - 1) + merged.shape[1:])
    own_part = reduce_partials(
        merged, "req", req_count, list(range(nb - 1, 0, -1)), [b for b in reduce_order if b != 0]
    )

    query_own = queries.reshape(SAMPLE_COUNT, DECODE_TOKENS, kv_local, query_groups, HEAD_SIZE)
    tail_key_block = sample_tail_keys.reshape(SAMPLE_COUNT, TAIL_LENGTH, kv_local, HEAD_SIZE)
    tail_value_block = sample_tail_values.reshape(SAMPLE_COUNT, TAIL_LENGTH, kv_local, HEAD_SIZE)
    fresh_k = fresh_rotated_keys.reshape(SAMPLE_COUNT, DECODE_TOKENS, kv_local, HEAD_SIZE)
    fresh_v = fresh_value_rows.reshape(SAMPLE_COUNT, DECODE_TOKENS, kv_local, HEAD_SIZE)
    score_tail = (
        jnp.einsum(
            "sjkgh,stkh->ksjgt", query_own, tail_key_block, preferred_element_type=jnp.float32
        )
        * inv_root
    )
    score_new = (
        jnp.einsum("sjkgh,sikh->ksjgi", query_own, fresh_k, preferred_element_type=jnp.float32)
        * inv_root
    )
    mask_tail = (jnp.arange(TAIL_LENGTH)[None, :] < sample_tail_length[0][:, None])[
        None, :, None, None, :
    ]
    causal = (jnp.arange(DECODE_TOKENS)[None, :] <= jnp.arange(DECODE_TOKENS)[:, None])[
        None, None, :, None, :
    ]
    local_top = jnp.maximum(
        jnp.max(jnp.where(mask_tail, score_tail, low), -1),
        jnp.max(jnp.where(causal, score_new, low), -1),
    )
    w_tail = jnp.where(mask_tail, jnp.exp(score_tail - local_top[..., None]), 0.0)
    w_new = jnp.where(causal, jnp.exp(score_new - local_top[..., None]), 0.0)
    local_sum = jnp.sum(w_tail, -1) + jnp.sum(w_new, -1)
    local_out = jnp.einsum(
        "ksjgt,stkh->ksjgh",
        w_tail.astype(jnp.bfloat16),
        tail_value_block,
        preferred_element_type=jnp.float32,
    )
    local_out = local_out + jnp.einsum(
        "ksjgi,sikh->ksjgh", w_new.astype(jnp.bfloat16), fresh_v, preferred_element_type=jnp.float32
    )
    lead = (kv_local, SAMPLE_COUNT, DECODE_TOKENS, query_groups)
    source_out = jnp.transpose(own_part[:HEAD_SIZE].reshape((HEAD_SIZE,) + lead), (1, 2, 3, 4, 0))
    source_top = own_part[HEAD_SIZE].reshape(lead)
    source_sum = own_part[HEAD_SIZE + 1].reshape(lead)
    overall = jnp.maximum(source_top, local_top)
    source_w = jnp.exp(source_top - overall)
    local_w = jnp.exp(local_top - overall)
    numer = source_w[..., None] * source_out + local_w[..., None] * local_out
    denom = source_w * source_sum + local_w * local_sum
    attention_layer = (numer / denom[..., None]).astype(jnp.bfloat16)
    attention_layer = jnp.transpose(attention_layer, (1, 2, 0, 3, 4)).reshape(
        SAMPLE_COUNT * DECODE_TOKENS, kv_local * query_groups * HEAD_SIZE
    )
    projected = jnp.dot(attention_layer, out_weight, preferred_element_type=jnp.float32)
    mlp_index = lax.axis_index("mlp")
    share = D // mlp_count
    mlp_orders = [[4, 1, 3], [1, 3, 4]] if mlp_count == 8 else [[1 << b for b in range(mlp_bits)]]
    mid = residual_in.astype(jnp.float32) + allreduce_bf16(
        projected, req_count, mlp_count, mlp_orders
    ).astype(jnp.float32)
    normed = (mid * rms_scale(jnp.sum(mid * mid, -1, keepdims=True), D) * mlp_gain).astype(
        jnp.bfloat16
    )
    gate = jnp.dot(normed, gate_weight, preferred_element_type=jnp.float32)
    upper = jnp.dot(normed, up_weight, preferred_element_type=jnp.float32)
    hidden = (jax.nn.silu(gate) * upper).astype(jnp.bfloat16)
    stream = mid + allreduce_bf16(
        jnp.dot(hidden, down_weight, preferred_element_type=jnp.float32), req_count, mlp_count, mlp_orders
    ).astype(jnp.float32)
    score = jnp.sum(
        stream
        * rms_scale(jnp.sum(stream * stream, -1, keepdims=True), D)
        * final_gain
        * score_weight,
        -1,
    )
    layer_out = lax.dynamic_slice_in_dim(stream, mlp_index * share, share, 1).astype(jnp.bfloat16)
    return (layer_out, score)


def solution(mesh):
    placed = (
        P("req", None),
        P("req", "mlp"),
        P("req", "mlp"),
        P("req", "mlp"),
        P(None, "req", "mlp"),
        P(None, "req", "mlp"),
        P("req", None, None, "mlp"),
        P("req", None, None, "mlp"),
        P(),
        P("req", None),
        P("mlp", None),
        P(None, "mlp"),
        P(None, "mlp"),
        P("mlp", None),
        P(),
        P(),
        P(),
    )
    return jax.shard_map(
        on_device,
        mesh=mesh,
        in_specs=placed,
        out_specs=(P("req", "mlp"), P("req")),
        check_vma=False,
    )
```

```python
import jax
import jax.numpy as jnp
from jax import lax
from jax.experimental import pallas as pl
from jax.experimental.pallas import tpu as pltpu
from jax.sharding import PartitionSpec as P

D = 2560
QUERY_HEADS = 32
KEY_VALUE_HEADS = 8
HEAD_SIZE = 80
SAMPLE_COUNT = 16
DECODE_TOKENS = 2
TAIL_LENGTH = 128


PACK = 88
BLOCK_PROMPTS = 8


def prefix_kernel(count_ref, half_ref, q_ref, kt_ref, vt_ref, out_ref):
    step = pl.program_id(0)
    rows = q_ref.shape[1]
    length = kt_ref.shape[2]

    def one(i, masked):
        q = q_ref[i]
        kt = kt_ref[i]
        vt = vt_ref[i]
        s = jnp.dot(q, kt, preferred_element_type=jnp.float32) * (HEAD_SIZE ** -0.5)
        if masked:
            place = lax.broadcasted_iota(jnp.int32, s.shape, 1)
            valid = place < count_ref[2 * (step * q_ref.shape[0] + i) + half_ref[0]]
            s = jnp.where(valid, s, jnp.float32(-1e30))
        top = jnp.max(s, axis=1, keepdims=True)
        w = jnp.exp(s - top)
        if masked:
            w = jnp.where(valid, w, 0.0)
        total = jnp.sum(w, axis=1, keepdims=True)
        o = lax.dot_general(vt, w.astype(jnp.bfloat16), (((1,), (1,)), ((), ())),
                            preferred_element_type=jnp.float32)
        lane = lax.broadcasted_iota(jnp.int32, (rows, 128), 1)
        stats = jnp.where(lane == 0, top, jnp.where(lane == 1, total, 0.0))
        out_ref[i, 0:HEAD_SIZE, :] = o
        out_ref[i, HEAD_SIZE:PACK, :] = jnp.transpose(stats)[0:PACK - HEAD_SIZE, :]

    for i in range(q_ref.shape[0]):
        count = count_ref[2 * (step * q_ref.shape[0] + i) + half_ref[0]]

        @pl.when(count >= length)
        def _():
            one(i, False)

        @pl.when(jnp.logical_and(count > 0, count < length))
        def _():
            one(i, True)

        @pl.when(count <= 0)
        def _():
            row = lax.broadcasted_iota(jnp.int32, (PACK, rows), 0)
            out_ref[i] = jnp.where(row == HEAD_SIZE, jnp.float32(-1e30), 0.0)


def prefix_partials(count, half, q, kt, vt):
    pairs, _, rows, _ = q.shape
    L = kt.shape[3]
    bp = min(BLOCK_PROMPTS, pairs)
    return pl.pallas_call(
        prefix_kernel,
        grid_spec=pltpu.PrefetchScalarGridSpec(
            num_scalar_prefetch=2,
            grid=(pairs // bp,),
            in_specs=[
                pl.BlockSpec((bp, None, rows, HEAD_SIZE), lambda p, c, h: (p, h[0], 0, 0)),
                pl.BlockSpec((bp, None, HEAD_SIZE, L), lambda p, c, h: (p, h[0], 0, 0)),
                pl.BlockSpec((bp, None, HEAD_SIZE, L), lambda p, c, h: (p, h[0], 0, 0)),
            ],
            out_specs=pl.BlockSpec((bp, PACK, rows), lambda p, c, h: (p, 0, 0)),
        ),
        out_shape=jax.ShapeDtypeStruct((pairs, PACK, rows), jnp.float32),
        cost_estimate=pl.CostEstimate(flops=4 * pairs * rows * L * HEAD_SIZE, transcendentals=pairs * rows * L,
                                      bytes_accessed=2 * pairs * L * HEAD_SIZE * 2 + pairs * rows * HEAD_SIZE * 2 + pairs * PACK * rows * 4),
    )(count, half, q, kt, vt)


def rms_scale(total_sq, width):
    return lax.rsqrt(total_sq / width + 1e-05)


def exchange(x, axis, n, bit):
    return lax.ppermute(x, axis, perm=[(i, i ^ (1 << bit)) for i in range(n)])


def gather_rows(x, axis, n, bits):
    me = lax.axis_index(axis)
    buf = x[None]
    taken = []
    for b in bits:
        other = exchange(buf, axis, n, b)
        high = ((me >> b) & 1) == 1
        buf = jnp.stack([jnp.where(high, other, buf), jnp.where(high, buf, other)])
        taken.insert(0, b)
    nb = len(bits)
    order = sorted(range(nb), key=lambda i: -taken[i])
    buf = jnp.transpose(buf, order + list(range(nb, buf.ndim)))
    return buf.reshape((n * x.shape[0],) + x.shape[1:])


def merge_partials(a, b):
    ma = a[..., HEAD_SIZE:HEAD_SIZE + 1, :]
    mb = b[..., HEAD_SIZE:HEAD_SIZE + 1, :]
    top = jnp.maximum(ma, mb)
    wa = jnp.exp(ma - top)
    wb = jnp.exp(mb - top)
    outs = a[..., :HEAD_SIZE, :] * wa + b[..., :HEAD_SIZE, :] * wb
    sums = a[..., HEAD_SIZE + 1:, :] * wa + b[..., HEAD_SIZE + 1:, :] * wb
    return jnp.concatenate([outs, top, sums], axis=-2)


def encode_partials(x):
    stats = x[..., HEAD_SIZE:HEAD_SIZE + 2, :]
    hi = lax.reduce_precision(stats, exponent_bits=8, mantissa_bits=7)
    rest = stats - hi
    mid = lax.reduce_precision(rest, exponent_bits=8, mantissa_bits=7)
    lo = rest - mid
    pad = jnp.zeros(x.shape[:-2] + (PACK - HEAD_SIZE - 6, x.shape[-1]), jnp.float32)
    return jnp.concatenate([x[..., :HEAD_SIZE, :], hi, mid, lo, pad], axis=-2).astype(jnp.bfloat16)


def decode_partials(y):
    y = y.astype(jnp.float32)
    base = HEAD_SIZE
    stats = (y[..., base:base + 2, :] + y[..., base + 2:base + 4, :]) + y[..., base + 4:base + 6, :]
    pad = jnp.zeros(y.shape[:-2] + (PACK - HEAD_SIZE - 2, y.shape[-1]), jnp.float32)
    return jnp.concatenate([y[..., :HEAD_SIZE, :], stats, pad], axis=-2)


def reduce_partials(cur, axis, n, left, bits):
    me = lax.axis_index(axis)
    left = list(left)
    for b in bits:
        ax = left.index(b)
        own = (me >> b) & 1
        keep = lax.dynamic_index_in_dim(cur, own, ax, keepdims=False)
        send = lax.dynamic_index_in_dim(cur, 1 - own, ax, keepdims=False)
        got = decode_partials(exchange(encode_partials(send), axis, n, b))
        cur = merge_partials(keep, got)
        left.remove(b)
    return cur


def allreduce_bf16(x, req_count, mlp_count, orders):
    cur = x.astype(jnp.bfloat16)
    for k in range(len(orders[0])):
        perm = []
        for r in range(req_count):
            mask = orders[r % len(orders)][k]
            perm += [(r * mlp_count + m, r * mlp_count + (m ^ mask)) for m in range(mlp_count)]
        other = lax.ppermute(cur, ("req", "mlp"), perm=perm)
        cur = (cur.astype(jnp.float32) + other.astype(jnp.float32)).astype(jnp.bfloat16)
    return cur


def on_device(
    residual_in,
    queries,
    fresh_rotated_keys,
    fresh_value_rows,
    shared_prefix_keys,
    shared_prefix_values,
    sample_tail_keys,
    sample_tail_values,
    prompt_prefix_length,
    sample_tail_length,
    out_weight,
    gate_weight,
    up_weight,
    down_weight,
    mlp_gain,
    final_gain,
    score_weight,
):
    query_groups = QUERY_HEADS // KEY_VALUE_HEADS
    inv_root = HEAD_SIZE ** (-0.5)
    kv_local = fresh_rotated_keys.shape[1] // HEAD_SIZE
    prompts = shared_prefix_keys.shape[0]
    piece_len = shared_prefix_keys.shape[1]
    req_count = lax.axis_size("req")
    req_bits = req_count.bit_length() - 1
    mlp_count = lax.axis_size("mlp")
    mlp_bits = mlp_count.bit_length() - 1
    req_index = lax.axis_index("req")
    low = jnp.float32(-1e30)
    rows = kv_local * SAMPLE_COUNT * DECODE_TOKENS * query_groups

    gather_order = [req_bits - 1] + ([1] if req_bits > 1 else []) + list(range(req_bits - 2, 1, -1)) + [0]
    gather_order = [b for i, b in enumerate(gather_order) if b not in gather_order[:i]]
    reduce_order = gather_order[::-1]

    gathered = gather_rows(queries, "req", req_count, gather_order)
    pairs = prompts // 2
    query_all = gathered.reshape(pairs, 2, rows, HEAD_SIZE)
    prefix_key_block = jnp.swapaxes(
        shared_prefix_keys.reshape(pairs, 2, piece_len, HEAD_SIZE * kv_local), 2, 3
    )
    prefix_value_block = jnp.swapaxes(
        shared_prefix_values.reshape(pairs, 2, piece_len, HEAD_SIZE * kv_local), 2, 3
    )
    count = jnp.clip(prompt_prefix_length - req_index * piece_len, 0, piece_len).astype(jnp.int32)
    own_low = (req_index & 1).astype(jnp.int32)
    send_half = prefix_partials(
        count, (1 - own_low)[None], query_all, prefix_key_block, prefix_value_block
    )
    got = exchange(send_half, "req", req_count, 0)
    keep_half = prefix_partials(count, own_low[None], query_all, prefix_key_block, prefix_value_block)
    merged = merge_partials(keep_half, got)
    nb = req_count.bit_length() - 1
    merged = merged.reshape((2,) * (nb - 1) + merged.shape[1:])
    own_part = reduce_partials(
        merged, "req", req_count, list(range(nb - 1, 0, -1)), [b for b in reduce_order if b != 0]
    )

    query_own = queries.reshape(SAMPLE_COUNT, DECODE_TOKENS, kv_local, query_groups, HEAD_SIZE)
    tail_key_block = sample_tail_keys.reshape(SAMPLE_COUNT, TAIL_LENGTH, kv_local, HEAD_SIZE)
    tail_value_block = sample_tail_values.reshape(SAMPLE_COUNT, TAIL_LENGTH, kv_local, HEAD_SIZE)
    fresh_k = fresh_rotated_keys.reshape(SAMPLE_COUNT, DECODE_TOKENS, kv_local, HEAD_SIZE)
    fresh_v = fresh_value_rows.reshape(SAMPLE_COUNT, DECODE_TOKENS, kv_local, HEAD_SIZE)
    score_tail = (
        jnp.einsum(
            "sjkgh,stkh->ksjgt", query_own, tail_key_block, preferred_element_type=jnp.float32
        )
        * inv_root
    )
    score_new = (
        jnp.einsum("sjkgh,sikh->ksjgi", query_own, fresh_k, preferred_element_type=jnp.float32)
        * inv_root
    )
    mask_tail = (jnp.arange(TAIL_LENGTH)[None, :] < sample_tail_length[0][:, None])[
        None, :, None, None, :
    ]
    causal = (jnp.arange(DECODE_TOKENS)[None, :] <= jnp.arange(DECODE_TOKENS)[:, None])[
        None, None, :, None, :
    ]
    local_top = jnp.maximum(
        jnp.max(jnp.where(mask_tail, score_tail, low), -1),
        jnp.max(jnp.where(causal, score_new, low), -1),
    )
    w_tail = jnp.where(mask_tail, jnp.exp(score_tail - local_top[..., None]), 0.0)
    w_new = jnp.where(causal, jnp.exp(score_new - local_top[..., None]), 0.0)
    local_sum = jnp.sum(w_tail, -1) + jnp.sum(w_new, -1)
    local_out = jnp.einsum(
        "ksjgt,stkh->ksjgh",
        w_tail.astype(jnp.bfloat16),
        tail_value_block,
        preferred_element_type=jnp.float32,
    )
    local_out = local_out + jnp.einsum(
        "ksjgi,sikh->ksjgh", w_new.astype(jnp.bfloat16), fresh_v, preferred_element_type=jnp.float32
    )
    lead = (kv_local, SAMPLE_COUNT, DECODE_TOKENS, query_groups)
    source_out = jnp.transpose(own_part[:HEAD_SIZE].reshape((HEAD_SIZE,) + lead), (1, 2, 3, 4, 0))
    source_top = own_part[HEAD_SIZE].reshape(lead)
    source_sum = own_part[HEAD_SIZE + 1].reshape(lead)
    overall = jnp.maximum(source_top, local_top)
    source_w = jnp.exp(source_top - overall)
    local_w = jnp.exp(local_top - overall)
    numer = source_w[..., None] * source_out + local_w[..., None] * local_out
    denom = source_w * source_sum + local_w * local_sum
    attention_layer = (numer / denom[..., None]).astype(jnp.bfloat16)
    attention_layer = jnp.transpose(attention_layer, (1, 2, 0, 3, 4)).reshape(
        SAMPLE_COUNT * DECODE_TOKENS, kv_local * query_groups * HEAD_SIZE
    )
    projected = jnp.dot(attention_layer, out_weight, preferred_element_type=jnp.float32)
    mlp_index = lax.axis_index("mlp")
    share = D // mlp_count
    mlp_orders = [[4, 1, 3], [1, 3, 4]] if mlp_count == 8 else [[1 << b for b in range(mlp_bits)]]
    mid = residual_in.astype(jnp.float32) + allreduce_bf16(
        projected, req_count, mlp_count, mlp_orders
    ).astype(jnp.float32)
    normed = (mid * rms_scale(jnp.sum(mid * mid, -1, keepdims=True), D) * mlp_gain).astype(
        jnp.bfloat16
    )
    gate = jnp.dot(normed, gate_weight, preferred_element_type=jnp.float32)
    upper = jnp.dot(normed, up_weight, preferred_element_type=jnp.float32)
    hidden = (jax.nn.silu(gate) * upper).astype(jnp.bfloat16)
    stream = mid + allreduce_bf16(
        jnp.dot(hidden, down_weight, preferred_element_type=jnp.float32), req_count, mlp_count, mlp_orders
    ).astype(jnp.float32)
    score = jnp.sum(
        stream
        * rms_scale(jnp.sum(stream * stream, -1, keepdims=True), D)
        * final_gain
        * score_weight,
        -1,
    )
    layer_out = lax.dynamic_slice_in_dim(stream, mlp_index * share, share, 1).astype(jnp.bfloat16)
    return (layer_out, score)


def solution(mesh):
    placed = (
        P("req", None),
        P("req", "mlp"),
        P("req", "mlp"),
        P("req", "mlp"),
        P(None, "req", "mlp"),
        P(None, "req", "mlp"),
        P("req", None, None, "mlp"),
        P("req", None, None, "mlp"),
        P(),
        P("req", None),
        P("mlp", None),
        P(None, "mlp"),
        P(None, "mlp"),
        P("mlp", None),
        P(),
        P(),
        P(),
    )
    return jax.shard_map(
        on_device,
        mesh=mesh,
        in_specs=placed,
        out_specs=(P("req", "mlp"), P("req")),
        check_vma=False,
    )
```

```python
import jax
import jax.numpy as jnp
from jax import lax
from jax.experimental import pallas as pl
from jax.experimental.pallas import tpu as pltpu
from jax.sharding import PartitionSpec as P

D = 2560
QUERY_HEADS = 32
KEY_VALUE_HEADS = 8
HEAD_SIZE = 80
SAMPLE_COUNT = 16
DECODE_TOKENS = 2
TAIL_LENGTH = 128


PACK = 88
BLOCK_PROMPTS = 8


def prefix_kernel(count_ref, half_ref, q_ref, kt_ref, vt_ref, out_ref):
    step = pl.program_id(0)
    for i in range(q_ref.shape[0]):
        q = q_ref[i]
        kt = kt_ref[i]
        vt = vt_ref[i]
        s = jnp.dot(q, kt, preferred_element_type=jnp.float32) * (HEAD_SIZE ** -0.5)
        place = lax.broadcasted_iota(jnp.int32, s.shape, 1)
        valid = place < count_ref[2 * (step * q_ref.shape[0] + i) + half_ref[0]]
        s = jnp.where(valid, s, jnp.float32(-1e30))
        top = jnp.max(s, axis=1, keepdims=True)
        w = jnp.where(valid, jnp.exp(s - top), 0.0)
        total = jnp.sum(w, axis=1, keepdims=True)
        o = lax.dot_general(vt, w.astype(jnp.bfloat16), (((1,), (1,)), ((), ())),
                            preferred_element_type=jnp.float32)
        lane = lax.broadcasted_iota(jnp.int32, (s.shape[0], 128), 1)
        stats = jnp.where(lane == 0, top, jnp.where(lane == 1, total, 0.0))
        out_ref[i, 0:HEAD_SIZE, :] = o
        out_ref[i, HEAD_SIZE:PACK, :] = jnp.transpose(stats)[0:PACK - HEAD_SIZE, :]


def prefix_partials(count, half, q, kt, vt):
    pairs, _, rows, _ = q.shape
    L = kt.shape[3]
    bp = min(BLOCK_PROMPTS, pairs)
    return pl.pallas_call(
        prefix_kernel,
        grid_spec=pltpu.PrefetchScalarGridSpec(
            num_scalar_prefetch=2,
            grid=(pairs // bp,),
            in_specs=[
                pl.BlockSpec((bp, None, rows, HEAD_SIZE), lambda p, c, h: (p, h[0], 0, 0)),
                pl.BlockSpec((bp, None, HEAD_SIZE, L), lambda p, c, h: (p, h[0], 0, 0)),
                pl.BlockSpec((bp, None, HEAD_SIZE, L), lambda p, c, h: (p, h[0], 0, 0)),
            ],
            out_specs=pl.BlockSpec((bp, PACK, rows), lambda p, c, h: (p, 0, 0)),
        ),
        out_shape=jax.ShapeDtypeStruct((pairs, PACK, rows), jnp.float32),
        cost_estimate=pl.CostEstimate(flops=4 * pairs * rows * L * HEAD_SIZE, transcendentals=pairs * rows * L,
                                      bytes_accessed=2 * pairs * L * HEAD_SIZE * 2 + pairs * rows * HEAD_SIZE * 2 + pairs * PACK * rows * 4),
    )(count, half, q, kt, vt)


def rms_scale(total_sq, width):
    return lax.rsqrt(total_sq / width + 1e-05)


def exchange(x, axis, n, bit):
    return lax.ppermute(x, axis, perm=[(i, i ^ (1 << bit)) for i in range(n)])


def gather_rows(x, axis, n, bits):
    me = lax.axis_index(axis)
    buf = x[None]
    taken = []
    for b in bits:
        other = exchange(buf, axis, n, b)
        high = ((me >> b) & 1) == 1
        buf = jnp.stack([jnp.where(high, other, buf), jnp.where(high, buf, other)])
        taken.insert(0, b)
    nb = len(bits)
    order = sorted(range(nb), key=lambda i: -taken[i])
    buf = jnp.transpose(buf, order + list(range(nb, buf.ndim)))
    return buf.reshape((n * x.shape[0],) + x.shape[1:])


def merge_partials(a, b):
    ma = a[..., HEAD_SIZE:HEAD_SIZE + 1, :]
    mb = b[..., HEAD_SIZE:HEAD_SIZE + 1, :]
    top = jnp.maximum(ma, mb)
    wa = jnp.exp(ma - top)
    wb = jnp.exp(mb - top)
    outs = a[..., :HEAD_SIZE, :] * wa + b[..., :HEAD_SIZE, :] * wb
    sums = a[..., HEAD_SIZE + 1:, :] * wa + b[..., HEAD_SIZE + 1:, :] * wb
    return jnp.concatenate([outs, top, sums], axis=-2)


def encode_partials(x):
    stats = x[..., HEAD_SIZE:HEAD_SIZE + 2, :]
    hi = lax.reduce_precision(stats, exponent_bits=8, mantissa_bits=7)
    rest = stats - hi
    mid = lax.reduce_precision(rest, exponent_bits=8, mantissa_bits=7)
    lo = rest - mid
    pad = jnp.zeros(x.shape[:-2] + (PACK - HEAD_SIZE - 6, x.shape[-1]), jnp.float32)
    return jnp.concatenate([x[..., :HEAD_SIZE, :], hi, mid, lo, pad], axis=-2).astype(jnp.bfloat16)


def decode_partials(y):
    y = y.astype(jnp.float32)
    base = HEAD_SIZE
    stats = (y[..., base:base + 2, :] + y[..., base + 2:base + 4, :]) + y[..., base + 4:base + 6, :]
    pad = jnp.zeros(y.shape[:-2] + (PACK - HEAD_SIZE - 2, y.shape[-1]), jnp.float32)
    return jnp.concatenate([y[..., :HEAD_SIZE, :], stats, pad], axis=-2)


def reduce_partials(cur, axis, n, left, bits):
    me = lax.axis_index(axis)
    left = list(left)
    for b in bits:
        ax = left.index(b)
        own = (me >> b) & 1
        keep = lax.dynamic_index_in_dim(cur, own, ax, keepdims=False)
        send = lax.dynamic_index_in_dim(cur, 1 - own, ax, keepdims=False)
        got = decode_partials(exchange(encode_partials(send), axis, n, b))
        cur = merge_partials(keep, got)
        left.remove(b)
    return cur


def allreduce_bf16(x, req_count, mlp_count, orders):
    cur = x.astype(jnp.bfloat16)
    for k in range(len(orders[0])):
        perm = []
        for r in range(req_count):
            mask = orders[r % len(orders)][k]
            perm += [(r * mlp_count + m, r * mlp_count + (m ^ mask)) for m in range(mlp_count)]
        other = lax.ppermute(cur, ("req", "mlp"), perm=perm)
        cur = (cur.astype(jnp.float32) + other.astype(jnp.float32)).astype(jnp.bfloat16)
    return cur


def on_device(
    residual_in,
    queries,
    fresh_rotated_keys,
    fresh_value_rows,
    shared_prefix_keys,
    shared_prefix_values,
    sample_tail_keys,
    sample_tail_values,
    prompt_prefix_length,
    sample_tail_length,
    out_weight,
    gate_weight,
    up_weight,
    down_weight,
    mlp_gain,
    final_gain,
    score_weight,
):
    query_groups = QUERY_HEADS // KEY_VALUE_HEADS
    inv_root = HEAD_SIZE ** (-0.5)
    kv_local = fresh_rotated_keys.shape[1] // HEAD_SIZE
    prompts = shared_prefix_keys.shape[0]
    piece_len = shared_prefix_keys.shape[1]
    req_count = lax.axis_size("req")
    req_bits = req_count.bit_length() - 1
    mlp_count = lax.axis_size("mlp")
    mlp_bits = mlp_count.bit_length() - 1
    req_index = lax.axis_index("req")
    low = jnp.float32(-1e30)
    rows = kv_local * SAMPLE_COUNT * DECODE_TOKENS * query_groups

    gather_order = [req_bits - 1] + ([1] if req_bits > 1 else []) + list(range(req_bits - 2, 1, -1)) + [0]
    gather_order = [b for i, b in enumerate(gather_order) if b not in gather_order[:i]]
    reduce_order = gather_order[::-1]

    query_own = queries.reshape(SAMPLE_COUNT, DECODE_TOKENS, kv_local, query_groups, HEAD_SIZE)
    tail_key_block = sample_tail_keys.reshape(SAMPLE_COUNT, TAIL_LENGTH, kv_local, HEAD_SIZE)
    tail_value_block = sample_tail_values.reshape(SAMPLE_COUNT, TAIL_LENGTH, kv_local, HEAD_SIZE)
    fresh_k = fresh_rotated_keys.reshape(SAMPLE_COUNT, DECODE_TOKENS, kv_local, HEAD_SIZE)
    fresh_v = fresh_value_rows.reshape(SAMPLE_COUNT, DECODE_TOKENS, kv_local, HEAD_SIZE)
    score_tail = (
        jnp.einsum(
            "sjkgh,stkh->ksjgt", query_own, tail_key_block, preferred_element_type=jnp.float32
        )
        * inv_root
    )
    score_new = (
        jnp.einsum("sjkgh,sikh->ksjgi", query_own, fresh_k, preferred_element_type=jnp.float32)
        * inv_root
    )
    mask_tail = (jnp.arange(TAIL_LENGTH)[None, :] < sample_tail_length[0][:, None])[
        None, :, None, None, :
    ]
    causal = (jnp.arange(DECODE_TOKENS)[None, :] <= jnp.arange(DECODE_TOKENS)[:, None])[
        None, None, :, None, :
    ]
    local_top = jnp.maximum(
        jnp.max(jnp.where(mask_tail, score_tail, low), -1),
        jnp.max(jnp.where(causal, score_new, low), -1),
    )
    w_tail = jnp.where(mask_tail, jnp.exp(score_tail - local_top[..., None]), 0.0)
    w_new = jnp.where(causal, jnp.exp(score_new - local_top[..., None]), 0.0)
    local_sum = jnp.sum(w_tail, -1) + jnp.sum(w_new, -1)
    local_out = jnp.einsum(
        "ksjgt,stkh->ksjgh",
        w_tail.astype(jnp.bfloat16),
        tail_value_block,
        preferred_element_type=jnp.float32,
    )
    local_out = local_out + jnp.einsum(
        "ksjgi,sikh->ksjgh", w_new.astype(jnp.bfloat16), fresh_v, preferred_element_type=jnp.float32
    )
    gathered = gather_rows(queries, "req", req_count, gather_order)
    gathered, local_out, local_top, local_sum = lax.optimization_barrier(
        (gathered, local_out, local_top, local_sum)
    )
    pairs = prompts // 2
    query_all = gathered.reshape(pairs, 2, rows, HEAD_SIZE)
    prefix_key_block = jnp.swapaxes(
        shared_prefix_keys.reshape(pairs, 2, piece_len, HEAD_SIZE * kv_local), 2, 3
    )
    prefix_value_block = jnp.swapaxes(
        shared_prefix_values.reshape(pairs, 2, piece_len, HEAD_SIZE * kv_local), 2, 3
    )
    count = jnp.clip(prompt_prefix_length - req_index * piece_len, 0, piece_len).astype(jnp.int32)
    own_low = (req_index & 1).astype(jnp.int32)
    send_half = prefix_partials(
        count, (1 - own_low)[None], query_all, prefix_key_block, prefix_value_block
    )
    got = exchange(send_half, "req", req_count, 0)
    keep_half = prefix_partials(count, own_low[None], query_all, prefix_key_block, prefix_value_block)
    merged = merge_partials(keep_half, got)
    nb = req_count.bit_length() - 1
    merged = merged.reshape((2,) * (nb - 1) + merged.shape[1:])
    own_part = reduce_partials(
        merged, "req", req_count, list(range(nb - 1, 0, -1)), [b for b in reduce_order if b != 0]
    )

    lead = (kv_local, SAMPLE_COUNT, DECODE_TOKENS, query_groups)
    source_out = jnp.transpose(own_part[:HEAD_SIZE].reshape((HEAD_SIZE,) + lead), (1, 2, 3, 4, 0))
    source_top = own_part[HEAD_SIZE].reshape(lead)
    source_sum = own_part[HEAD_SIZE + 1].reshape(lead)
    overall = jnp.maximum(source_top, local_top)
    source_w = jnp.exp(source_top - overall)
    local_w = jnp.exp(local_top - overall)
    numer = source_w[..., None] * source_out + local_w[..., None] * local_out
    denom = source_w * source_sum + local_w * local_sum
    attention_layer = (numer / denom[..., None]).astype(jnp.bfloat16)
    attention_layer = jnp.transpose(attention_layer, (1, 2, 0, 3, 4)).reshape(
        SAMPLE_COUNT * DECODE_TOKENS, kv_local * query_groups * HEAD_SIZE
    )
    projected = jnp.dot(attention_layer, out_weight, preferred_element_type=jnp.float32)
    mlp_index = lax.axis_index("mlp")
    share = D // mlp_count
    mlp_orders = [[4, 1, 3], [1, 3, 4]] if mlp_count == 8 else [[1 << b for b in range(mlp_bits)]]
    mid = residual_in.astype(jnp.float32) + allreduce_bf16(
        projected, req_count, mlp_count, mlp_orders
    ).astype(jnp.float32)
    normed = (mid * rms_scale(jnp.sum(mid * mid, -1, keepdims=True), D) * mlp_gain).astype(
        jnp.bfloat16
    )
    gate = jnp.dot(normed, gate_weight, preferred_element_type=jnp.float32)
    upper = jnp.dot(normed, up_weight, preferred_element_type=jnp.float32)
    hidden = (jax.nn.silu(gate) * upper).astype(jnp.bfloat16)
    stream = mid + allreduce_bf16(
        jnp.dot(hidden, down_weight, preferred_element_type=jnp.float32), req_count, mlp_count, mlp_orders
    ).astype(jnp.float32)
    score = jnp.sum(
        stream
        * rms_scale(jnp.sum(stream * stream, -1, keepdims=True), D)
        * final_gain
        * score_weight,
        -1,
    )
    layer_out = lax.dynamic_slice_in_dim(stream, mlp_index * share, share, 1).astype(jnp.bfloat16)
    return (layer_out, score)


def solution(mesh):
    placed = (
        P("req", None),
        P("req", "mlp"),
        P("req", "mlp"),
        P("req", "mlp"),
        P(None, "req", "mlp"),
        P(None, "req", "mlp"),
        P("req", None, None, "mlp"),
        P("req", None, None, "mlp"),
        P(),
        P("req", None),
        P("mlp", None),
        P(None, "mlp"),
        P(None, "mlp"),
        P("mlp", None),
        P(),
        P(),
        P(),
    )
    return jax.shard_map(
        on_device,
        mesh=mesh,
        in_specs=placed,
        out_specs=(P("req", "mlp"), P("req")),
        check_vma=False,
    )
```

```python
import jax
import jax.numpy as jnp
from jax import lax
from jax.experimental import pallas as pl
from jax.experimental.pallas import tpu as pltpu
from jax.sharding import PartitionSpec as P

D = 2560
QUERY_HEADS = 32
KEY_VALUE_HEADS = 8
HEAD_SIZE = 80
SAMPLE_COUNT = 16
DECODE_TOKENS = 2
TAIL_LENGTH = 128


PACK = 88
BLOCK_PROMPTS = 8


def prefix_kernel(count_ref, half_ref, q_ref, kt_ref, vt_ref, out_ref):
    step = pl.program_id(0)
    for i in range(q_ref.shape[0]):
        q = q_ref[i]
        kt = kt_ref[i]
        vt = vt_ref[i]
        s = jnp.dot(q, kt, preferred_element_type=jnp.float32) * (HEAD_SIZE ** -0.5)
        place = lax.broadcasted_iota(jnp.int32, s.shape, 1)
        valid = place < count_ref[2 * (step * q_ref.shape[0] + i) + half_ref[0]]
        s = jnp.where(valid, s, jnp.float32(-1e30))
        top = jnp.max(s, axis=1, keepdims=True)
        w = jnp.where(valid, jnp.exp(s - top), 0.0)
        total = jnp.sum(w, axis=1, keepdims=True)
        o = lax.dot_general(vt, w.astype(jnp.bfloat16), (((1,), (1,)), ((), ())),
                            preferred_element_type=jnp.float32)
        lane = lax.broadcasted_iota(jnp.int32, (s.shape[0], 128), 1)
        stats = jnp.where(lane == 0, top, jnp.where(lane == 1, total, 0.0))
        out_ref[i, 0:HEAD_SIZE, :] = o
        out_ref[i, HEAD_SIZE:PACK, :] = jnp.transpose(stats)[0:PACK - HEAD_SIZE, :]


def prefix_partials(count, half, q, kt, vt):
    pairs, _, rows, _ = q.shape
    L = kt.shape[3]
    bp = min(BLOCK_PROMPTS, pairs)
    return pl.pallas_call(
        prefix_kernel,
        grid_spec=pltpu.PrefetchScalarGridSpec(
            num_scalar_prefetch=2,
            grid=(pairs // bp,),
            in_specs=[
                pl.BlockSpec((bp, None, rows, HEAD_SIZE), lambda p, c, h: (p, h[0], 0, 0)),
                pl.BlockSpec((bp, None, HEAD_SIZE, L), lambda p, c, h: (p, h[0], 0, 0)),
                pl.BlockSpec((bp, None, HEAD_SIZE, L), lambda p, c, h: (p, h[0], 0, 0)),
            ],
            out_specs=pl.BlockSpec((bp, PACK, rows), lambda p, c, h: (p, 0, 0)),
        ),
        out_shape=jax.ShapeDtypeStruct((pairs, PACK, rows), jnp.float32),
        cost_estimate=pl.CostEstimate(flops=4 * pairs * rows * L * HEAD_SIZE, transcendentals=pairs * rows * L,
                                      bytes_accessed=2 * pairs * L * HEAD_SIZE * 2 + pairs * rows * HEAD_SIZE * 2 + pairs * PACK * rows * 4),
    )(count, half, q, kt, vt)


def rms_scale(total_sq, width):
    return lax.rsqrt(total_sq / width + 1e-05)


def exchange(x, axis, n, bit):
    return lax.ppermute(x, axis, perm=[(i, i ^ (1 << bit)) for i in range(n)])


def gather_rows(x, axis, n, bits, tie, tie_after):
    me = lax.axis_index(axis)
    buf = x[None]
    taken = []
    for b in bits:
        other = exchange(buf, axis, n, b)
        high = ((me >> b) & 1) == 1
        buf = jnp.stack([jnp.where(high, other, buf), jnp.where(high, buf, other)])
        taken.insert(0, b)
        if len(taken) == tie_after:
            buf, tie = lax.optimization_barrier((buf, tie))
    nb = len(bits)
    order = sorted(range(nb), key=lambda i: -taken[i])
    buf = jnp.transpose(buf, order + list(range(nb, buf.ndim)))
    return buf.reshape((n * x.shape[0],) + x.shape[1:]), tie


def merge_partials(a, b):
    ma = a[..., HEAD_SIZE:HEAD_SIZE + 1, :]
    mb = b[..., HEAD_SIZE:HEAD_SIZE + 1, :]
    top = jnp.maximum(ma, mb)
    wa = jnp.exp(ma - top)
    wb = jnp.exp(mb - top)
    outs = a[..., :HEAD_SIZE, :] * wa + b[..., :HEAD_SIZE, :] * wb
    sums = a[..., HEAD_SIZE + 1:, :] * wa + b[..., HEAD_SIZE + 1:, :] * wb
    return jnp.concatenate([outs, top, sums], axis=-2)


def encode_partials(x):
    stats = x[..., HEAD_SIZE:HEAD_SIZE + 2, :]
    hi = lax.reduce_precision(stats, exponent_bits=8, mantissa_bits=7)
    rest = stats - hi
    mid = lax.reduce_precision(rest, exponent_bits=8, mantissa_bits=7)
    lo = rest - mid
    pad = jnp.zeros(x.shape[:-2] + (PACK - HEAD_SIZE - 6, x.shape[-1]), jnp.float32)
    return jnp.concatenate([x[..., :HEAD_SIZE, :], hi, mid, lo, pad], axis=-2).astype(jnp.bfloat16)


def decode_partials(y):
    y = y.astype(jnp.float32)
    base = HEAD_SIZE
    stats = (y[..., base:base + 2, :] + y[..., base + 2:base + 4, :]) + y[..., base + 4:base + 6, :]
    pad = jnp.zeros(y.shape[:-2] + (PACK - HEAD_SIZE - 2, y.shape[-1]), jnp.float32)
    return jnp.concatenate([y[..., :HEAD_SIZE, :], stats, pad], axis=-2)


def reduce_partials(cur, axis, n, left, bits):
    me = lax.axis_index(axis)
    left = list(left)
    for b in bits:
        ax = left.index(b)
        own = (me >> b) & 1
        keep = lax.dynamic_index_in_dim(cur, own, ax, keepdims=False)
        send = lax.dynamic_index_in_dim(cur, 1 - own, ax, keepdims=False)
        got = decode_partials(exchange(encode_partials(send), axis, n, b))
        cur = merge_partials(keep, got)
        left.remove(b)
    return cur


def allreduce_bf16(x, req_count, mlp_count, orders):
    cur = x.astype(jnp.bfloat16)
    for k in range(len(orders[0])):
        perm = []
        for r in range(req_count):
            mask = orders[r % len(orders)][k]
            perm += [(r * mlp_count + m, r * mlp_count + (m ^ mask)) for m in range(mlp_count)]
        other = lax.ppermute(cur, ("req", "mlp"), perm=perm)
        cur = (cur.astype(jnp.float32) + other.astype(jnp.float32)).astype(jnp.bfloat16)
    return cur


def on_device(
    residual_in,
    queries,
    fresh_rotated_keys,
    fresh_value_rows,
    shared_prefix_keys,
    shared_prefix_values,
    sample_tail_keys,
    sample_tail_values,
    prompt_prefix_length,
    sample_tail_length,
    out_weight,
    gate_weight,
    up_weight,
    down_weight,
    mlp_gain,
    final_gain,
    score_weight,
):
    query_groups = QUERY_HEADS // KEY_VALUE_HEADS
    inv_root = HEAD_SIZE ** (-0.5)
    kv_local = fresh_rotated_keys.shape[1] // HEAD_SIZE
    prompts = shared_prefix_keys.shape[0]
    piece_len = shared_prefix_keys.shape[1]
    req_count = lax.axis_size("req")
    req_bits = req_count.bit_length() - 1
    mlp_count = lax.axis_size("mlp")
    mlp_bits = mlp_count.bit_length() - 1
    req_index = lax.axis_index("req")
    low = jnp.float32(-1e30)
    rows = kv_local * SAMPLE_COUNT * DECODE_TOKENS * query_groups

    gather_order = [req_bits - 1] + ([1] if req_bits > 1 else []) + list(range(req_bits - 2, 1, -1)) + [0]
    gather_order = [b for i, b in enumerate(gather_order) if b not in gather_order[:i]]
    reduce_order = gather_order[::-1]

    gathered, local_queries = gather_rows(queries, "req", req_count, gather_order, queries, 2)
    query_own = local_queries.reshape(SAMPLE_COUNT, DECODE_TOKENS, kv_local, query_groups, HEAD_SIZE)
    tail_key_block = sample_tail_keys.reshape(SAMPLE_COUNT, TAIL_LENGTH, kv_local, HEAD_SIZE)
    tail_value_block = sample_tail_values.reshape(SAMPLE_COUNT, TAIL_LENGTH, kv_local, HEAD_SIZE)
    fresh_k = fresh_rotated_keys.reshape(SAMPLE_COUNT, DECODE_TOKENS, kv_local, HEAD_SIZE)
    fresh_v = fresh_value_rows.reshape(SAMPLE_COUNT, DECODE_TOKENS, kv_local, HEAD_SIZE)
    score_tail = (
        jnp.einsum(
            "sjkgh,stkh->ksjgt", query_own, tail_key_block, preferred_element_type=jnp.float32
        )
        * inv_root
    )
    score_new = (
        jnp.einsum("sjkgh,sikh->ksjgi", query_own, fresh_k, preferred_element_type=jnp.float32)
        * inv_root
    )
    mask_tail = (jnp.arange(TAIL_LENGTH)[None, :] < sample_tail_length[0][:, None])[
        None, :, None, None, :
    ]
    causal = (jnp.arange(DECODE_TOKENS)[None, :] <= jnp.arange(DECODE_TOKENS)[:, None])[
        None, None, :, None, :
    ]
    local_top = jnp.maximum(
        jnp.max(jnp.where(mask_tail, score_tail, low), -1),
        jnp.max(jnp.where(causal, score_new, low), -1),
    )
    w_tail = jnp.where(mask_tail, jnp.exp(score_tail - local_top[..., None]), 0.0)
    w_new = jnp.where(causal, jnp.exp(score_new - local_top[..., None]), 0.0)
    local_sum = jnp.sum(w_tail, -1) + jnp.sum(w_new, -1)
    local_out = jnp.einsum(
        "ksjgt,stkh->ksjgh",
        w_tail.astype(jnp.bfloat16),
        tail_value_block,
        preferred_element_type=jnp.float32,
    )
    local_out = local_out + jnp.einsum(
        "ksjgi,sikh->ksjgh", w_new.astype(jnp.bfloat16), fresh_v, preferred_element_type=jnp.float32
    )
    gathered, local_out, local_top, local_sum = lax.optimization_barrier(
        (gathered, local_out, local_top, local_sum)
    )
    pairs = prompts // 2
    query_all = gathered.reshape(pairs, 2, rows, HEAD_SIZE)
    prefix_key_block = jnp.swapaxes(
        shared_prefix_keys.reshape(pairs, 2, piece_len, HEAD_SIZE * kv_local), 2, 3
    )
    prefix_value_block = jnp.swapaxes(
        shared_prefix_values.reshape(pairs, 2, piece_len, HEAD_SIZE * kv_local), 2, 3
    )
    count = jnp.clip(prompt_prefix_length - req_index * piece_len, 0, piece_len).astype(jnp.int32)
    own_low = (req_index & 1).astype(jnp.int32)
    send_half = prefix_partials(
        count, (1 - own_low)[None], query_all, prefix_key_block, prefix_value_block
    )
    got = exchange(send_half, "req", req_count, 0)
    keep_half = prefix_partials(count, own_low[None], query_all, prefix_key_block, prefix_value_block)
    merged = merge_partials(keep_half, got)
    nb = req_count.bit_length() - 1
    merged = merged.reshape((2,) * (nb - 1) + merged.shape[1:])
    own_part = reduce_partials(
        merged, "req", req_count, list(range(nb - 1, 0, -1)), [b for b in reduce_order if b != 0]
    )

    lead = (kv_local, SAMPLE_COUNT, DECODE_TOKENS, query_groups)
    source_out = jnp.transpose(own_part[:HEAD_SIZE].reshape((HEAD_SIZE,) + lead), (1, 2, 3, 4, 0))
    source_top = own_part[HEAD_SIZE].reshape(lead)
    source_sum = own_part[HEAD_SIZE + 1].reshape(lead)
    overall = jnp.maximum(source_top, local_top)
    source_w = jnp.exp(source_top - overall)
    local_w = jnp.exp(local_top - overall)
    numer = source_w[..., None] * source_out + local_w[..., None] * local_out
    denom = source_w * source_sum + local_w * local_sum
    attention_layer = (numer / denom[..., None]).astype(jnp.bfloat16)
    attention_layer = jnp.transpose(attention_layer, (1, 2, 0, 3, 4)).reshape(
        SAMPLE_COUNT * DECODE_TOKENS, kv_local * query_groups * HEAD_SIZE
    )
    projected = jnp.dot(attention_layer, out_weight, preferred_element_type=jnp.float32)
    mlp_index = lax.axis_index("mlp")
    share = D // mlp_count
    mlp_orders = [[4, 1, 3], [1, 3, 4]] if mlp_count == 8 else [[1 << b for b in range(mlp_bits)]]
    mid = residual_in.astype(jnp.float32) + allreduce_bf16(
        projected, req_count, mlp_count, mlp_orders
    ).astype(jnp.float32)
    normed = (mid * rms_scale(jnp.sum(mid * mid, -1, keepdims=True), D) * mlp_gain).astype(
        jnp.bfloat16
    )
    gate = jnp.dot(normed, gate_weight, preferred_element_type=jnp.float32)
    upper = jnp.dot(normed, up_weight, preferred_element_type=jnp.float32)
    hidden = (jax.nn.silu(gate) * upper).astype(jnp.bfloat16)
    stream = mid + allreduce_bf16(
        jnp.dot(hidden, down_weight, preferred_element_type=jnp.float32), req_count, mlp_count, mlp_orders
    ).astype(jnp.float32)
    score = jnp.sum(
        stream
        * rms_scale(jnp.sum(stream * stream, -1, keepdims=True), D)
        * final_gain
        * score_weight,
        -1,
    )
    layer_out = lax.dynamic_slice_in_dim(stream, mlp_index * share, share, 1).astype(jnp.bfloat16)
    return (layer_out, score)


def solution(mesh):
    placed = (
        P("req", None),
        P("req", "mlp"),
        P("req", "mlp"),
        P("req", "mlp"),
        P(None, "req", "mlp"),
        P(None, "req", "mlp"),
        P("req", None, None, "mlp"),
        P("req", None, None, "mlp"),
        P(),
        P("req", None),
        P("mlp", None),
        P(None, "mlp"),
        P(None, "mlp"),
        P("mlp", None),
        P(),
        P(),
        P(),
    )
    return jax.shard_map(
        on_device,
        mesh=mesh,
        in_specs=placed,
        out_specs=(P("req", "mlp"), P("req")),
        check_vma=False,
    )
```

```python
import jax
import jax.numpy as jnp
from jax import lax
from jax.experimental import pallas as pl
from jax.experimental.pallas import tpu as pltpu
from jax.sharding import PartitionSpec as P

D = 2560
QUERY_HEADS = 32
KEY_VALUE_HEADS = 8
HEAD_SIZE = 80
SAMPLE_COUNT = 16
DECODE_TOKENS = 2
TAIL_LENGTH = 128


PACK = 88
BLOCK_PROMPTS = 8


def prefix_kernel(count_ref, half_ref, q_ref, kt_ref, vt_ref, out_ref):
    step = pl.program_id(0)
    for i in range(q_ref.shape[0]):
        q = q_ref[i]
        kt = kt_ref[i]
        vt = vt_ref[i]
        s = jnp.dot(q, kt, preferred_element_type=jnp.float32) * (HEAD_SIZE ** -0.5)
        place = lax.broadcasted_iota(jnp.int32, s.shape, 1)
        valid = place < count_ref[2 * (step * q_ref.shape[0] + i) + half_ref[0]]
        s = jnp.where(valid, s, jnp.float32(-1e30))
        top = jnp.max(s, axis=1, keepdims=True)
        w = jnp.where(valid, jnp.exp(s - top), 0.0)
        total = jnp.sum(w, axis=1, keepdims=True)
        o = lax.dot_general(vt, w.astype(jnp.bfloat16), (((1,), (1,)), ((), ())),
                            preferred_element_type=jnp.float32)
        lane = lax.broadcasted_iota(jnp.int32, (s.shape[0], 128), 1)
        stats = jnp.where(lane == 0, top, jnp.where(lane == 1, total, 0.0))
        out_ref[i, 0:HEAD_SIZE, :] = o
        out_ref[i, HEAD_SIZE:PACK, :] = jnp.transpose(stats)[0:PACK - HEAD_SIZE, :]


def prefix_partials(count, half, q, kt, vt):
    pairs, rows, _ = q.shape
    L = kt.shape[3]
    bp = min(BLOCK_PROMPTS, pairs)
    return pl.pallas_call(
        prefix_kernel,
        grid_spec=pltpu.PrefetchScalarGridSpec(
            num_scalar_prefetch=2,
            grid=(pairs // bp,),
            in_specs=[
                pl.BlockSpec((bp, rows, HEAD_SIZE), lambda p, c, h: (p, 0, 0)),
                pl.BlockSpec((bp, None, HEAD_SIZE, L), lambda p, c, h: (p, h[0], 0, 0)),
                pl.BlockSpec((bp, None, HEAD_SIZE, L), lambda p, c, h: (p, h[0], 0, 0)),
            ],
            out_specs=pl.BlockSpec((bp, PACK, rows), lambda p, c, h: (p, 0, 0)),
        ),
        out_shape=jax.ShapeDtypeStruct((pairs, PACK, rows), jnp.float32),
        cost_estimate=pl.CostEstimate(flops=4 * pairs * rows * L * HEAD_SIZE, transcendentals=pairs * rows * L,
                                      bytes_accessed=2 * pairs * L * HEAD_SIZE * 2 + pairs * rows * HEAD_SIZE * 2 + pairs * PACK * rows * 4),
    )(count, half, q, kt, vt)


def rms_scale(total_sq, width):
    return lax.rsqrt(total_sq / width + 1e-05)


def exchange(x, axis, n, bit):
    return lax.ppermute(x, axis, perm=[(i, i ^ (1 << bit)) for i in range(n)])


def gather_rows(x, axis, n, bits, tie, tie_after):
    me = lax.axis_index(axis)
    buf = x[None]
    taken = []
    for b in bits:
        other = exchange(buf, axis, n, b)
        high = ((me >> b) & 1) == 1
        buf = jnp.stack([jnp.where(high, other, buf), jnp.where(high, buf, other)])
        taken.insert(0, b)
        if len(taken) == tie_after:
            buf, tie = lax.optimization_barrier((buf, tie))
    nb = len(bits)
    order = sorted(range(nb), key=lambda i: -taken[i])
    buf = jnp.transpose(buf, order + list(range(nb, buf.ndim)))
    return buf.reshape((n * x.shape[0],) + x.shape[1:]), tie


def gather_halves(x, axis, n, bits, tie, tie_after):
    me = lax.axis_index(axis)
    buf = x[None]
    taken = []
    for b in bits[:-1]:
        other = exchange(buf, axis, n, b)
        high = ((me >> b) & 1) == 1
        buf = jnp.stack([jnp.where(high, other, buf), jnp.where(high, buf, other)])
        taken.insert(0, b)
        if len(taken) == tie_after:
            buf, tie = lax.optimization_barrier((buf, tie))
    other = exchange(buf, axis, n, bits[-1])
    nb = len(taken)
    order = sorted(range(nb), key=lambda i: -taken[i])
    shape = ((n // 2) * x.shape[0],) + x.shape[1:]

    def arrange(y):
        return jnp.transpose(y, order + list(range(nb, y.ndim))).reshape(shape)

    return arrange(buf), arrange(other), tie


def merge_partials(a, b):
    ma = a[..., HEAD_SIZE:HEAD_SIZE + 1, :]
    mb = b[..., HEAD_SIZE:HEAD_SIZE + 1, :]
    top = jnp.maximum(ma, mb)
    wa = jnp.exp(ma - top)
    wb = jnp.exp(mb - top)
    outs = a[..., :HEAD_SIZE, :] * wa + b[..., :HEAD_SIZE, :] * wb
    sums = a[..., HEAD_SIZE + 1:, :] * wa + b[..., HEAD_SIZE + 1:, :] * wb
    return jnp.concatenate([outs, top, sums], axis=-2)


def encode_partials(x):
    stats = x[..., HEAD_SIZE:HEAD_SIZE + 2, :]
    hi = lax.reduce_precision(stats, exponent_bits=8, mantissa_bits=7)
    rest = stats - hi
    mid = lax.reduce_precision(rest, exponent_bits=8, mantissa_bits=7)
    lo = rest - mid
    pad = jnp.zeros(x.shape[:-2] + (PACK - HEAD_SIZE - 6, x.shape[-1]), jnp.float32)
    return jnp.concatenate([x[..., :HEAD_SIZE, :], hi, mid, lo, pad], axis=-2).astype(jnp.bfloat16)


def decode_partials(y):
    y = y.astype(jnp.float32)
    base = HEAD_SIZE
    stats = (y[..., base:base + 2, :] + y[..., base + 2:base + 4, :]) + y[..., base + 4:base + 6, :]
    pad = jnp.zeros(y.shape[:-2] + (PACK - HEAD_SIZE - 2, y.shape[-1]), jnp.float32)
    return jnp.concatenate([y[..., :HEAD_SIZE, :], stats, pad], axis=-2)


def reduce_partials(cur, axis, n, left, bits):
    me = lax.axis_index(axis)
    left = list(left)
    for b in bits:
        ax = left.index(b)
        own = (me >> b) & 1
        keep = lax.dynamic_index_in_dim(cur, own, ax, keepdims=False)
        send = lax.dynamic_index_in_dim(cur, 1 - own, ax, keepdims=False)
        got = decode_partials(exchange(encode_partials(send), axis, n, b))
        cur = merge_partials(keep, got)
        left.remove(b)
    return cur


def allreduce_bf16(x, req_count, mlp_count, orders):
    cur = x.astype(jnp.bfloat16)
    for k in range(len(orders[0])):
        perm = []
        for r in range(req_count):
            mask = orders[r % len(orders)][k]
            perm += [(r * mlp_count + m, r * mlp_count + (m ^ mask)) for m in range(mlp_count)]
        other = lax.ppermute(cur, ("req", "mlp"), perm=perm)
        cur = (cur.astype(jnp.float32) + other.astype(jnp.float32)).astype(jnp.bfloat16)
    return cur


def on_device(
    residual_in,
    queries,
    fresh_rotated_keys,
    fresh_value_rows,
    shared_prefix_keys,
    shared_prefix_values,
    sample_tail_keys,
    sample_tail_values,
    prompt_prefix_length,
    sample_tail_length,
    out_weight,
    gate_weight,
    up_weight,
    down_weight,
    mlp_gain,
    final_gain,
    score_weight,
):
    query_groups = QUERY_HEADS // KEY_VALUE_HEADS
    inv_root = HEAD_SIZE ** (-0.5)
    kv_local = fresh_rotated_keys.shape[1] // HEAD_SIZE
    prompts = shared_prefix_keys.shape[0]
    piece_len = shared_prefix_keys.shape[1]
    req_count = lax.axis_size("req")
    req_bits = req_count.bit_length() - 1
    mlp_count = lax.axis_size("mlp")
    mlp_bits = mlp_count.bit_length() - 1
    req_index = lax.axis_index("req")
    low = jnp.float32(-1e30)
    rows = kv_local * SAMPLE_COUNT * DECODE_TOKENS * query_groups

    gather_order = [req_bits - 1] + ([1] if req_bits > 1 else []) + list(range(req_bits - 2, 1, -1)) + [0]
    gather_order = [b for i, b in enumerate(gather_order) if b not in gather_order[:i]]
    reduce_order = gather_order[::-1]

    assert gather_order[-1] == 0
    own_queries, other_queries, local_queries = gather_halves(
        queries, "req", req_count, gather_order, queries, 2
    )
    query_own = local_queries.reshape(SAMPLE_COUNT, DECODE_TOKENS, kv_local, query_groups, HEAD_SIZE)
    tail_key_block = sample_tail_keys.reshape(SAMPLE_COUNT, TAIL_LENGTH, kv_local, HEAD_SIZE)
    tail_value_block = sample_tail_values.reshape(SAMPLE_COUNT, TAIL_LENGTH, kv_local, HEAD_SIZE)
    fresh_k = fresh_rotated_keys.reshape(SAMPLE_COUNT, DECODE_TOKENS, kv_local, HEAD_SIZE)
    fresh_v = fresh_value_rows.reshape(SAMPLE_COUNT, DECODE_TOKENS, kv_local, HEAD_SIZE)
    score_tail = (
        jnp.einsum(
            "sjkgh,stkh->ksjgt", query_own, tail_key_block, preferred_element_type=jnp.float32
        )
        * inv_root
    )
    score_new = (
        jnp.einsum("sjkgh,sikh->ksjgi", query_own, fresh_k, preferred_element_type=jnp.float32)
        * inv_root
    )
    mask_tail = (jnp.arange(TAIL_LENGTH)[None, :] < sample_tail_length[0][:, None])[
        None, :, None, None, :
    ]
    causal = (jnp.arange(DECODE_TOKENS)[None, :] <= jnp.arange(DECODE_TOKENS)[:, None])[
        None, None, :, None, :
    ]
    local_top = jnp.maximum(
        jnp.max(jnp.where(mask_tail, score_tail, low), -1),
        jnp.max(jnp.where(causal, score_new, low), -1),
    )
    w_tail = jnp.where(mask_tail, jnp.exp(score_tail - local_top[..., None]), 0.0)
    w_new = jnp.where(causal, jnp.exp(score_new - local_top[..., None]), 0.0)
    local_sum = jnp.sum(w_tail, -1) + jnp.sum(w_new, -1)
    local_out = jnp.einsum(
        "ksjgt,stkh->ksjgh",
        w_tail.astype(jnp.bfloat16),
        tail_value_block,
        preferred_element_type=jnp.float32,
    )
    local_out = local_out + jnp.einsum(
        "ksjgi,sikh->ksjgh", w_new.astype(jnp.bfloat16), fresh_v, preferred_element_type=jnp.float32
    )
    own_queries, other_queries, local_out, local_top, local_sum = lax.optimization_barrier(
        (own_queries, other_queries, local_out, local_top, local_sum)
    )
    pairs = prompts // 2
    query_keep = own_queries.reshape(pairs, rows, HEAD_SIZE)
    query_send = other_queries.reshape(pairs, rows, HEAD_SIZE)
    prefix_key_block = jnp.swapaxes(
        shared_prefix_keys.reshape(pairs, 2, piece_len, HEAD_SIZE * kv_local), 2, 3
    )
    prefix_value_block = jnp.swapaxes(
        shared_prefix_values.reshape(pairs, 2, piece_len, HEAD_SIZE * kv_local), 2, 3
    )
    count = jnp.clip(prompt_prefix_length - req_index * piece_len, 0, piece_len).astype(jnp.int32)
    own_low = (req_index & 1).astype(jnp.int32)
    send_half = prefix_partials(
        count, (1 - own_low)[None], query_send, prefix_key_block, prefix_value_block
    )
    got = exchange(send_half, "req", req_count, 0)
    keep_half = prefix_partials(count, own_low[None], query_keep, prefix_key_block, prefix_value_block)
    merged = merge_partials(keep_half, got)
    nb = req_count.bit_length() - 1
    merged = merged.reshape((2,) * (nb - 1) + merged.shape[1:])
    own_part = reduce_partials(
        merged, "req", req_count, list(range(nb - 1, 0, -1)), [b for b in reduce_order if b != 0]
    )

    lead = (kv_local, SAMPLE_COUNT, DECODE_TOKENS, query_groups)
    source_out = jnp.transpose(own_part[:HEAD_SIZE].reshape((HEAD_SIZE,) + lead), (1, 2, 3, 4, 0))
    source_top = own_part[HEAD_SIZE].reshape(lead)
    source_sum = own_part[HEAD_SIZE + 1].reshape(lead)
    overall = jnp.maximum(source_top, local_top)
    source_w = jnp.exp(source_top - overall)
    local_w = jnp.exp(local_top - overall)
    numer = source_w[..., None] * source_out + local_w[..., None] * local_out
    denom = source_w * source_sum + local_w * local_sum
    attention_layer = (numer / denom[..., None]).astype(jnp.bfloat16)
    attention_layer = jnp.transpose(attention_layer, (1, 2, 0, 3, 4)).reshape(
        SAMPLE_COUNT * DECODE_TOKENS, kv_local * query_groups * HEAD_SIZE
    )
    projected = jnp.dot(attention_layer, out_weight, preferred_element_type=jnp.float32)
    mlp_index = lax.axis_index("mlp")
    share = D // mlp_count
    mlp_orders = [[4, 1, 3], [1, 3, 4]] if mlp_count == 8 else [[1 << b for b in range(mlp_bits)]]
    mid = residual_in.astype(jnp.float32) + allreduce_bf16(
        projected, req_count, mlp_count, mlp_orders
    ).astype(jnp.float32)
    normed = (mid * rms_scale(jnp.sum(mid * mid, -1, keepdims=True), D) * mlp_gain).astype(
        jnp.bfloat16
    )
    gate = jnp.dot(normed, gate_weight, preferred_element_type=jnp.float32)
    upper = jnp.dot(normed, up_weight, preferred_element_type=jnp.float32)
    hidden = (jax.nn.silu(gate) * upper).astype(jnp.bfloat16)
    stream = mid + allreduce_bf16(
        jnp.dot(hidden, down_weight, preferred_element_type=jnp.float32), req_count, mlp_count, mlp_orders
    ).astype(jnp.float32)
    score = jnp.sum(
        stream
        * rms_scale(jnp.sum(stream * stream, -1, keepdims=True), D)
        * final_gain
        * score_weight,
        -1,
    )
    layer_out = lax.dynamic_slice_in_dim(stream, mlp_index * share, share, 1).astype(jnp.bfloat16)
    return (layer_out, score)


def solution(mesh):
    placed = (
        P("req", None),
        P("req", "mlp"),
        P("req", "mlp"),
        P("req", "mlp"),
        P(None, "req", "mlp"),
        P(None, "req", "mlp"),
        P("req", None, None, "mlp"),
        P("req", None, None, "mlp"),
        P(),
        P("req", None),
        P("mlp", None),
        P(None, "mlp"),
        P(None, "mlp"),
        P("mlp", None),
        P(),
        P(),
        P(),
    )
    return jax.shard_map(
        on_device,
        mesh=mesh,
        in_specs=placed,
        out_specs=(P("req", "mlp"), P("req")),
        check_vma=False,
    )
```

```python
import jax
import jax.numpy as jnp
from jax import lax
from jax.experimental import pallas as pl
from jax.experimental.pallas import tpu as pltpu
from jax.sharding import PartitionSpec as P

D = 2560
QUERY_HEADS = 32
KEY_VALUE_HEADS = 8
HEAD_SIZE = 80
SAMPLE_COUNT = 16
DECODE_TOKENS = 2
TAIL_LENGTH = 128


PACK = 88
BLOCK_PROMPTS = 16


def prefix_kernel(count_ref, half_ref, q_ref, kt_ref, vt_ref, out_ref):
    step = pl.program_id(0)
    for i in range(q_ref.shape[0]):
        q = q_ref[i]
        kt = kt_ref[i]
        vt = vt_ref[i]
        s = jnp.dot(q, kt, preferred_element_type=jnp.float32) * (HEAD_SIZE ** -0.5)
        place = lax.broadcasted_iota(jnp.int32, s.shape, 1)
        valid = place < count_ref[2 * (step * q_ref.shape[0] + i) + half_ref[0]]
        s = jnp.where(valid, s, jnp.float32(-1e30))
        top = jnp.max(s, axis=1, keepdims=True)
        w = jnp.where(valid, jnp.exp(s - top), 0.0)
        total = jnp.sum(w, axis=1, keepdims=True)
        o = lax.dot_general(vt, w.astype(jnp.bfloat16), (((1,), (1,)), ((), ())),
                            preferred_element_type=jnp.float32)
        lane = lax.broadcasted_iota(jnp.int32, (s.shape[0], 128), 1)
        stats = jnp.where(lane == 0, top, jnp.where(lane == 1, total, 0.0))
        out_ref[i, 0:HEAD_SIZE, :] = o
        out_ref[i, HEAD_SIZE:PACK, :] = jnp.transpose(stats)[0:PACK - HEAD_SIZE, :]


def prefix_partials(count, half, q, kt, vt):
    pairs, _, rows, _ = q.shape
    L = kt.shape[3]
    bp = min(BLOCK_PROMPTS, pairs)
    return pl.pallas_call(
        prefix_kernel,
        grid_spec=pltpu.PrefetchScalarGridSpec(
            num_scalar_prefetch=2,
            grid=(pairs // bp,),
            in_specs=[
                pl.BlockSpec((bp, None, rows, HEAD_SIZE), lambda p, c, h: (p, h[0], 0, 0)),
                pl.BlockSpec((bp, None, HEAD_SIZE, L), lambda p, c, h: (p, h[0], 0, 0)),
                pl.BlockSpec((bp, None, HEAD_SIZE, L), lambda p, c, h: (p, h[0], 0, 0)),
            ],
            out_specs=pl.BlockSpec((bp, PACK, rows), lambda p, c, h: (p, 0, 0)),
        ),
        out_shape=jax.ShapeDtypeStruct((pairs, PACK, rows), jnp.float32),
        cost_estimate=pl.CostEstimate(flops=4 * pairs * rows * L * HEAD_SIZE, transcendentals=pairs * rows * L,
                                      bytes_accessed=2 * pairs * L * HEAD_SIZE * 2 + pairs * rows * HEAD_SIZE * 2 + pairs * PACK * rows * 4),
    )(count, half, q, kt, vt)


def rms_scale(total_sq, width):
    return lax.rsqrt(total_sq / width + 1e-05)


def exchange(x, axis, n, bit):
    return lax.ppermute(x, axis, perm=[(i, i ^ (1 << bit)) for i in range(n)])


def gather_rows(x, axis, n, bits, tie, tie_after):
    me = lax.axis_index(axis)
    buf = x[None]
    taken = []
    for b in bits:
        other = exchange(buf, axis, n, b)
        high = ((me >> b) & 1) == 1
        buf = jnp.stack([jnp.where(high, other, buf), jnp.where(high, buf, other)])
        taken.insert(0, b)
        if len(taken) == tie_after:
            buf, tie = lax.optimization_barrier((buf, tie))
    nb = len(bits)
    order = sorted(range(nb), key=lambda i: -taken[i])
    buf = jnp.transpose(buf, order + list(range(nb, buf.ndim)))
    return buf.reshape((n * x.shape[0],) + x.shape[1:]), tie


def merge_partials(a, b):
    ma = a[..., HEAD_SIZE:HEAD_SIZE + 1, :]
    mb = b[..., HEAD_SIZE:HEAD_SIZE + 1, :]
    top = jnp.maximum(ma, mb)
    wa = jnp.exp(ma - top)
    wb = jnp.exp(mb - top)
    outs = a[..., :HEAD_SIZE, :] * wa + b[..., :HEAD_SIZE, :] * wb
    sums = a[..., HEAD_SIZE + 1:, :] * wa + b[..., HEAD_SIZE + 1:, :] * wb
    return jnp.concatenate([outs, top, sums], axis=-2)


def encode_partials(x):
    stats = x[..., HEAD_SIZE:HEAD_SIZE + 2, :]
    hi = lax.reduce_precision(stats, exponent_bits=8, mantissa_bits=7)
    rest = stats - hi
    mid = lax.reduce_precision(rest, exponent_bits=8, mantissa_bits=7)
    lo = rest - mid
    pad = jnp.zeros(x.shape[:-2] + (PACK - HEAD_SIZE - 6, x.shape[-1]), jnp.float32)
    return jnp.concatenate([x[..., :HEAD_SIZE, :], hi, mid, lo, pad], axis=-2).astype(jnp.bfloat16)


def decode_partials(y):
    y = y.astype(jnp.float32)
    base = HEAD_SIZE
    stats = (y[..., base:base + 2, :] + y[..., base + 2:base + 4, :]) + y[..., base + 4:base + 6, :]
    pad = jnp.zeros(y.shape[:-2] + (PACK - HEAD_SIZE - 2, y.shape[-1]), jnp.float32)
    return jnp.concatenate([y[..., :HEAD_SIZE, :], stats, pad], axis=-2)


def reduce_partials(cur, axis, n, left, bits):
    me = lax.axis_index(axis)
    left = list(left)
    for b in bits:
        ax = left.index(b)
        own = (me >> b) & 1
        keep = lax.dynamic_index_in_dim(cur, own, ax, keepdims=False)
        send = lax.dynamic_index_in_dim(cur, 1 - own, ax, keepdims=False)
        got = decode_partials(exchange(encode_partials(send), axis, n, b))
        cur = merge_partials(keep, got)
        left.remove(b)
    return cur


def allreduce_bf16(x, req_count, mlp_count, orders):
    cur = x.astype(jnp.bfloat16)
    for k in range(len(orders[0])):
        perm = []
        for r in range(req_count):
            mask = orders[r % len(orders)][k]
            perm += [(r * mlp_count + m, r * mlp_count + (m ^ mask)) for m in range(mlp_count)]
        other = lax.ppermute(cur, ("req", "mlp"), perm=perm)
        cur = (cur.astype(jnp.float32) + other.astype(jnp.float32)).astype(jnp.bfloat16)
    return cur


def on_device(
    residual_in,
    queries,
    fresh_rotated_keys,
    fresh_value_rows,
    shared_prefix_keys,
    shared_prefix_values,
    sample_tail_keys,
    sample_tail_values,
    prompt_prefix_length,
    sample_tail_length,
    out_weight,
    gate_weight,
    up_weight,
    down_weight,
    mlp_gain,
    final_gain,
    score_weight,
):
    query_groups = QUERY_HEADS // KEY_VALUE_HEADS
    inv_root = HEAD_SIZE ** (-0.5)
    kv_local = fresh_rotated_keys.shape[1] // HEAD_SIZE
    prompts = shared_prefix_keys.shape[0]
    piece_len = shared_prefix_keys.shape[1]
    req_count = lax.axis_size("req")
    req_bits = req_count.bit_length() - 1
    mlp_count = lax.axis_size("mlp")
    mlp_bits = mlp_count.bit_length() - 1
    req_index = lax.axis_index("req")
    low = jnp.float32(-1e30)
    rows = kv_local * SAMPLE_COUNT * DECODE_TOKENS * query_groups

    gather_order = [req_bits - 1] + ([1] if req_bits > 1 else []) + list(range(req_bits - 2, 1, -1)) + [0]
    gather_order = [b for i, b in enumerate(gather_order) if b not in gather_order[:i]]
    reduce_order = gather_order[::-1]

    gathered, local_queries = gather_rows(queries, "req", req_count, gather_order, queries, 2)
    query_own = local_queries.reshape(SAMPLE_COUNT, DECODE_TOKENS, kv_local, query_groups, HEAD_SIZE)
    tail_key_block = sample_tail_keys.reshape(SAMPLE_COUNT, TAIL_LENGTH, kv_local, HEAD_SIZE)
    tail_value_block = sample_tail_values.reshape(SAMPLE_COUNT, TAIL_LENGTH, kv_local, HEAD_SIZE)
    fresh_k = fresh_rotated_keys.reshape(SAMPLE_COUNT, DECODE_TOKENS, kv_local, HEAD_SIZE)
    fresh_v = fresh_value_rows.reshape(SAMPLE_COUNT, DECODE_TOKENS, kv_local, HEAD_SIZE)
    score_tail = (
        jnp.einsum(
            "sjkgh,stkh->ksjgt", query_own, tail_key_block, preferred_element_type=jnp.float32
        )
        * inv_root
    )
    score_new = (
        jnp.einsum("sjkgh,sikh->ksjgi", query_own, fresh_k, preferred_element_type=jnp.float32)
        * inv_root
    )
    mask_tail = (jnp.arange(TAIL_LENGTH)[None, :] < sample_tail_length[0][:, None])[
        None, :, None, None, :
    ]
    causal = (jnp.arange(DECODE_TOKENS)[None, :] <= jnp.arange(DECODE_TOKENS)[:, None])[
        None, None, :, None, :
    ]
    local_top = jnp.maximum(
        jnp.max(jnp.where(mask_tail, score_tail, low), -1),
        jnp.max(jnp.where(causal, score_new, low), -1),
    )
    w_tail = jnp.where(mask_tail, jnp.exp(score_tail - local_top[..., None]), 0.0)
    w_new = jnp.where(causal, jnp.exp(score_new - local_top[..., None]), 0.0)
    local_sum = jnp.sum(w_tail, -1) + jnp.sum(w_new, -1)
    local_out = jnp.einsum(
        "ksjgt,stkh->ksjgh",
        w_tail.astype(jnp.bfloat16),
        tail_value_block,
        preferred_element_type=jnp.float32,
    )
    local_out = local_out + jnp.einsum(
        "ksjgi,sikh->ksjgh", w_new.astype(jnp.bfloat16), fresh_v, preferred_element_type=jnp.float32
    )
    gathered, local_out, local_top, local_sum = lax.optimization_barrier(
        (gathered, local_out, local_top, local_sum)
    )
    pairs = prompts // 2
    query_all = gathered.reshape(pairs, 2, rows, HEAD_SIZE)
    prefix_key_block = jnp.swapaxes(
        shared_prefix_keys.reshape(pairs, 2, piece_len, HEAD_SIZE * kv_local), 2, 3
    )
    prefix_value_block = jnp.swapaxes(
        shared_prefix_values.reshape(pairs, 2, piece_len, HEAD_SIZE * kv_local), 2, 3
    )
    count = jnp.clip(prompt_prefix_length - req_index * piece_len, 0, piece_len).astype(jnp.int32)
    own_low = (req_index & 1).astype(jnp.int32)
    send_half = prefix_partials(
        count, (1 - own_low)[None], query_all, prefix_key_block, prefix_value_block
    )
    got = exchange(send_half, "req", req_count, 0)
    keep_half = prefix_partials(count, own_low[None], query_all, prefix_key_block, prefix_value_block)
    merged = merge_partials(keep_half, got)
    nb = req_count.bit_length() - 1
    merged = merged.reshape((2,) * (nb - 1) + merged.shape[1:])
    own_part = reduce_partials(
        merged, "req", req_count, list(range(nb - 1, 0, -1)), [b for b in reduce_order if b != 0]
    )

    lead = (kv_local, SAMPLE_COUNT, DECODE_TOKENS, query_groups)
    source_out = jnp.transpose(own_part[:HEAD_SIZE].reshape((HEAD_SIZE,) + lead), (1, 2, 3, 4, 0))
    source_top = own_part[HEAD_SIZE].reshape(lead)
    source_sum = own_part[HEAD_SIZE + 1].reshape(lead)
    overall = jnp.maximum(source_top, local_top)
    source_w = jnp.exp(source_top - overall)
    local_w = jnp.exp(local_top - overall)
    numer = source_w[..., None] * source_out + local_w[..., None] * local_out
    denom = source_w * source_sum + local_w * local_sum
    attention_layer = (numer / denom[..., None]).astype(jnp.bfloat16)
    attention_layer = jnp.transpose(attention_layer, (1, 2, 0, 3, 4)).reshape(
        SAMPLE_COUNT * DECODE_TOKENS, kv_local * query_groups * HEAD_SIZE
    )
    projected = jnp.dot(attention_layer, out_weight, preferred_element_type=jnp.float32)
    mlp_index = lax.axis_index("mlp")
    share = D // mlp_count
    mlp_orders = [[4, 1, 3], [1, 3, 4]] if mlp_count == 8 else [[1 << b for b in range(mlp_bits)]]
    mid = residual_in.astype(jnp.float32) + allreduce_bf16(
        projected, req_count, mlp_count, mlp_orders
    ).astype(jnp.float32)
    normed = (mid * rms_scale(jnp.sum(mid * mid, -1, keepdims=True), D) * mlp_gain).astype(
        jnp.bfloat16
    )
    gate = jnp.dot(normed, gate_weight, preferred_element_type=jnp.float32)
    upper = jnp.dot(normed, up_weight, preferred_element_type=jnp.float32)
    hidden = (jax.nn.silu(gate) * upper).astype(jnp.bfloat16)
    stream = mid + allreduce_bf16(
        jnp.dot(hidden, down_weight, preferred_element_type=jnp.float32), req_count, mlp_count, mlp_orders
    ).astype(jnp.float32)
    score = jnp.sum(
        stream
        * rms_scale(jnp.sum(stream * stream, -1, keepdims=True), D)
        * final_gain
        * score_weight,
        -1,
    )
    layer_out = lax.dynamic_slice_in_dim(stream, mlp_index * share, share, 1).astype(jnp.bfloat16)
    return (layer_out, score)


def solution(mesh):
    placed = (
        P("req", None),
        P("req", "mlp"),
        P("req", "mlp"),
        P("req", "mlp"),
        P(None, "req", "mlp"),
        P(None, "req", "mlp"),
        P("req", None, None, "mlp"),
        P("req", None, None, "mlp"),
        P(),
        P("req", None),
        P("mlp", None),
        P(None, "mlp"),
        P(None, "mlp"),
        P("mlp", None),
        P(),
        P(),
        P(),
    )
    return jax.shard_map(
        on_device,
        mesh=mesh,
        in_specs=placed,
        out_specs=(P("req", "mlp"), P("req")),
        check_vma=False,
    )
```
